512 devices in a mesh: seq: 128 (over z_hi, x, y), dp: 4 (over z_lo, core).
Axes of the slice: x: 4, y: 8, z: 8 (z_hi: 4, z_lo: 2; z = z_hi * 2 + z_lo), core: 2. Of those that a mesh axis runs over, the one named last changes fastest.
Arguments:
- query_proj: bfloat16 [4, 16384, 2048], P('dp', 'seq'), may hold values from -48 to 48
- key_projection: bfloat16 [4, 16384, 1024], P('dp', 'seq'), may hold values from -48 to 48
- value_proj: bfloat16 [4, 16384, 1024], P('dp', 'seq'), may hold values from -6 to 6
- attn_grad: bfloat16 [4, 16384, 2048], P('dp', 'seq'), may hold values from -6 to 6
- doc_ids: int32 [4, 16384], P('dp', 'seq'), may hold values from 0 to 8, as said below
- query_gain: float32 [128], replicated, may hold values from 0.5 to 1.5
- key_norm_gain: float32 [128], replicated, may hold values from 0.5 to 1.5
Outputs:
- query_grad: bfloat16 [4, 16384, 2048], P('dp', 'seq')
- key_grad: bfloat16 [4, 16384, 1024], P('dp', 'seq')
- value_grad: bfloat16 [4, 16384, 1024], P('dp', 'seq')
- query_gain_grad: float32 [128], replicated
- key_gain_grad: float32 [128], replicated
The draws below stay inside these ranges and needn't reach their ends.
Inputs may be any that keep to these rules, and one draw needn't show every extreme that they name: `doc_ids`: document numbers never fall along a sequence and each is used; each document holds 1 to 2175 tokens, and one holds exactly 2175.
All inputs are finite; a program needn't handle non-finite values.
Results may differ from the reference program's by a relative error of at most 0.008.
Values may be sent and summed in bfloat16 or wider, within the bound.
No kernel may reach another device: no remote copies, remote signals or barrier semaphores. Data moves between devices by JAX's collectives and lax.ppermute only.
A program may use at most 128 MiB of HBM per device.

```python
import math
import jax
import jax.numpy as jnp
from jax import lax

HEAD_SIZE = 128
QUERY_HEADS = 16
KEY_VALUE_HEADS = 8
WINDOW_LENGTH = 1024
TOK_DEV = 128
QW = 2048
KVW = 1024
SEQS = 4
SEQUENCE_TOKENS = 16384
DOCS = 9


def rows_scaled(key, heads):
    base_key, row_key, col_key = jax.random.split(key, 3)
    shape = (SEQS, SEQUENCE_TOKENS, heads, HEAD_SIZE)
    base = jnp.clip(jax.random.normal(base_key, shape, jnp.float32), -4.0, 4.0)
    row_scale = jnp.exp(jax.random.uniform(row_key, (SEQS, SEQUENCE_TOKENS, heads, 1), jnp.float32, math.log(0.3), math.log(3.0)))
    col_scale = jnp.exp(jax.random.uniform(col_key, (1, 1, 1, HEAD_SIZE), jnp.float32, math.log(0.4), math.log(4.0)))
    return (base * row_scale * col_scale).reshape(SEQS, SEQUENCE_TOKENS, heads * HEAD_SIZE).astype(jnp.bfloat16)


def draw_query_proj(key, part):
    return rows_scaled(jax.random.fold_in(key, 11), QUERY_HEADS)


def draw_key_projection(key, part):
    return rows_scaled(jax.random.fold_in(key, 12), KEY_VALUE_HEADS)


def draw_doc_ids(key, part):
    groups = DOCS - 1
    stride_len = SEQUENCE_TOKENS // groups
    middle = groups // 2
    slab_count = SEQUENCE_TOKENS // TOK_DEV
    index_row = jnp.arange(groups - 1, dtype=jnp.int32)
    jitter = jax.random.randint(jax.random.fold_in(key, 13), (SEQS, groups - 1), 0, TOK_DEV, dtype=jnp.int32)
    middle_jitter = jax.random.randint(jax.random.fold_in(key, 14), (SEQS, 1), 1, TOK_DEV, dtype=jnp.int32)
    jitter = jnp.where(index_row[None, :] == middle - 1, middle_jitter, jitter)
    choosable = [c for c in range(groups - 1) if c != middle - 1 and c != middle]
    picked = jnp.array(choosable, dtype=jnp.int32)[jax.random.randint(jax.random.fold_in(key, 15), (SEQS,), 0, len(choosable), dtype=jnp.int32)]
    jitter = jnp.where(index_row[None, :] == picked[:, None], TOK_DEV - 1, jitter)
    jitter = jnp.where(index_row[None, :] == picked[:, None] - 1, 0, jitter)
    bounds = ((index_row + 1) * stride_len)[None, :] + jitter
    extra = (slab_count // 2 - 1) * TOK_DEV + jax.random.randint(jax.random.fold_in(key, 16), (SEQS, 1), 0, TOK_DEV, dtype=jnp.int32)
    bounds = jnp.concatenate([bounds, extra], axis=1)
    places = jnp.arange(SEQUENCE_TOKENS, dtype=jnp.int32)
    return jnp.sum((places[None, :, None] >= bounds[:, None, :]).astype(jnp.int32), axis=-1).astype(jnp.int32)


def steps_of(stream_key, extent, cuts, smallest, top_value):
    def one(position, parts):
        steps = jax.random.uniform(jax.random.fold_in(jax.random.fold_in(stream_key, 6), position), (parts,), jnp.float32, smallest / len(cuts), top_value / len(cuts))
        return jnp.repeat(jnp.exp(steps), extent[position] // parts).reshape((-1,) + (1,) * (len(extent) - position - 1))

    factor_of = one(*cuts[0])
    for cut in cuts[1:]:
        factor_of = factor_of * one(*cut)
    return factor_of


def noise(rng, dims, scale, reach, cuts=(), kind=jnp.bfloat16):
    drawn = jax.random.normal(rng, dims, jnp.float32) * scale
    if len(cuts) > 0:
        drawn = steps_of(rng, dims, cuts, -0.22, 0.18) * drawn
    return jnp.clip(drawn, min=-reach, max=reach).astype(kind)


def setup_inputs(seed: int = 0) -> dict:
    key_of = jax.random.split(jax.random.key(seed), 8)
    return {
        "query_proj": draw_query_proj(jax.random.fold_in(key_of[7], 71), 0),
        "key_projection": draw_key_projection(jax.random.fold_in(key_of[7], 71), 0),
        "value_proj": noise(key_of[2], (SEQS, SEQUENCE_TOKENS, KVW), 1.0, 6.0, ((0, 4), (1, 128))),
        "attn_grad": noise(key_of[3], (SEQS, SEQUENCE_TOKENS, QW), 1.0, 6.0, ((0, 4), (1, 128))),
        "doc_ids": draw_doc_ids(jax.random.fold_in(key_of[7], 71), 0),
        "query_gain": jnp.clip(1.0 + 0.1 * jax.random.normal(key_of[5], (HEAD_SIZE,), jnp.float32), 0.5, 1.5),
        "key_norm_gain": jnp.clip(1.0 + 0.1 * jax.random.normal(key_of[6], (HEAD_SIZE,), jnp.float32), 0.5, 1.5),
    }


rope_base = 10000.0
score_scale = 168.0 ** (-0.5)
norm_eps = 1e-06

def rotary(field, positions):
    half = field.shape[-1] // 2
    freqs = rope_base ** (-jnp.arange(half, dtype=field.dtype) * 2.0 / field.shape[-1])
    angles = positions.astype(field.dtype)[:, None] * freqs[None, :]
    cosine = jnp.cos(angles)[:, None, :]
    sine = jnp.sin(angles)[:, None, :]
    first = field[..., :half]
    second = field[..., half:]
    return jnp.concatenate([first * cosine - second * sine, second * cosine + first * sine], axis=-1)

def prepare(raw, gain, positions):
    meansq = lax.optimization_barrier(jnp.mean(raw * raw, axis=-1, keepdims=True))
    normed = raw * lax.rsqrt(meansq + norm_eps) * gain
    return rotary(normed, positions)

def round_remote(part):
    remote = lax.optimization_barrier(part[:WINDOW_LENGTH].astype(jnp.bfloat16)).astype(part.dtype)
    return jnp.concatenate([remote, part[WINDOW_LENGTH:]], axis=0)

def attend(query_blk, key_blk, value_blk, gradient_block, allowed):
    query_f = query_blk.astype(jnp.float32)
    key_f = key_blk.astype(jnp.float32)
    value_f = value_blk.astype(jnp.float32)
    gradient_float = gradient_block.astype(jnp.float32)
    scores = jnp.einsum('tgrd,wgd->grtw', query_f, key_f) * score_scale
    expd = jnp.where(allowed, jnp.exp(scores), 0.0)
    weights = expd / lax.optimization_barrier(jnp.sum(expd, axis=-1, keepdims=True))
    weights_b = lax.optimization_barrier(weights.astype(jnp.bfloat16)).astype(jnp.float32)
    attention_probs = jnp.einsum('grtw,wgd->tgrd', weights_b, value_f)
    delta_rows = jnp.einsum('jwkp,jwkp->wkj', gradient_float, attention_probs)
    dweights = jnp.einsum('tgrd,wgd->grtw', gradient_float, value_f)
    dscores = lax.optimization_barrier((weights * (dweights - delta_rows[..., None])).astype(jnp.bfloat16)).astype(jnp.float32)
    dquery = score_scale * jnp.einsum('grtw,wgd->tgrd', dscores, key_f)
    dkey = score_scale * jnp.einsum('grtw,tgrd->wgd', dscores, query_f)
    dvalue = jnp.einsum('grtw,tgrd->wgd', weights_b, gradient_float)
    return (dquery, dkey, dvalue)

def reference(query_proj, key_projection, value_proj, attn_grad, doc_ids, query_gain, key_norm_gain):
    group_ratio = QUERY_HEADS // KEY_VALUE_HEADS
    span = WINDOW_LENGTH + TOK_DEV

    def one_sequence(items):
        query_in, key_input, value_input, gradient_input, doc_row = items
        positions = jnp.arange(SEQUENCE_TOKENS, dtype=jnp.int32)
        starts = jnp.searchsorted(doc_row, doc_row, side='left').astype(jnp.int32)

        def prepare_function(raw, gain):
            return prepare(raw, gain, positions)
        query_normalized, query_back = jax.vjp(prepare_function, query_in.astype(jnp.float32).reshape(SEQUENCE_TOKENS, QUERY_HEADS, HEAD_SIZE), query_gain)
        key_normalized, key_backward = jax.vjp(prepare_function, key_input.astype(jnp.float32).reshape(SEQUENCE_TOKENS, KEY_VALUE_HEADS, HEAD_SIZE), key_norm_gain)
        query_every_head = query_normalized.astype(jnp.bfloat16).reshape(SEQUENCE_TOKENS, KEY_VALUE_HEADS, group_ratio, HEAD_SIZE)
        gradient_total = gradient_input.reshape(SEQUENCE_TOKENS, KEY_VALUE_HEADS, group_ratio, HEAD_SIZE)
        padding_rows = jnp.zeros((WINDOW_LENGTH, KEY_VALUE_HEADS, HEAD_SIZE), jnp.bfloat16)
        key_pad = jnp.concatenate([padding_rows, key_normalized.astype(jnp.bfloat16)], axis=0)
        value_padded = jnp.concatenate([padding_rows, value_input.reshape(SEQUENCE_TOKENS, KEY_VALUE_HEADS, HEAD_SIZE)], axis=0)

        def block_step(carry, index):
            key_acc, value_accumulator = carry
            begin = (index * TOK_DEV).astype(jnp.int32)
            query_blk = lax.dynamic_slice_in_dim(query_every_head, begin, TOK_DEV, 0)
            gradient_block = lax.dynamic_slice_in_dim(gradient_total, begin, TOK_DEV, 0)
            key_blk = lax.dynamic_slice_in_dim(key_pad, begin, span, 0)
            value_blk = lax.dynamic_slice_in_dim(value_padded, begin, span, 0)
            query_pos = begin + jnp.arange(TOK_DEV, dtype=jnp.int32)
            key_pos = begin - WINDOW_LENGTH + jnp.arange(span, dtype=jnp.int32)
            query_start = lax.dynamic_slice_in_dim(starts, begin, TOK_DEV, 0)
            allowed = (key_pos[None, :] <= query_pos[:, None]) & (query_pos[:, None] - key_pos[None, :] < WINDOW_LENGTH) & (key_pos[None, :] >= query_start[:, None])
            dquery, dkey, dvalue = attend(query_blk, key_blk, value_blk, gradient_block, allowed)
            dkey = round_remote(dkey)
            dvalue = round_remote(dvalue)
            key_acc = lax.dynamic_update_slice_in_dim(key_acc, lax.dynamic_slice_in_dim(key_acc, begin, span, 0) + dkey, begin, 0)
            value_accumulator = lax.dynamic_update_slice_in_dim(value_accumulator, lax.dynamic_slice_in_dim(value_accumulator, begin, span, 0) + dvalue, begin, 0)
            return ((key_acc, value_accumulator), dquery)
        zero_filled = jnp.zeros((WINDOW_LENGTH + SEQUENCE_TOKENS, KEY_VALUE_HEADS, HEAD_SIZE), jnp.float32)
        (key_acc, value_accumulator), dquery_blocks = lax.scan(block_step, (zero_filled, zero_filled), jnp.arange(SEQUENCE_TOKENS // TOK_DEV, dtype=jnp.int32))
        dquery_rot = dquery_blocks.reshape(SEQUENCE_TOKENS, QUERY_HEADS, HEAD_SIZE)
        query_raw_gradient, query_gain_gradient = query_back(dquery_rot)
        key_raw_gradient, key_gain_gradient = key_backward(key_acc[WINDOW_LENGTH:])
        return (query_raw_gradient.astype(jnp.bfloat16).reshape(SEQUENCE_TOKENS, QUERY_HEADS * HEAD_SIZE), key_raw_gradient.astype(jnp.bfloat16).reshape(SEQUENCE_TOKENS, KEY_VALUE_HEADS * HEAD_SIZE), value_accumulator[WINDOW_LENGTH:].astype(jnp.bfloat16).reshape(SEQUENCE_TOKENS, KEY_VALUE_HEADS * HEAD_SIZE), query_gain_gradient, key_gain_gradient)
    results = lax.map(one_sequence, (query_proj, key_projection, value_proj, attn_grad, doc_ids))
    return (results[0], results[1], results[2], lax.optimization_barrier(jnp.sum(results[3], axis=0)), lax.optimization_barrier(jnp.sum(results[4], axis=0)))
```

```python
import jax
import jax.numpy as jnp
from jax import lax
from jax.sharding import PartitionSpec as P

HEAD_SIZE = 128
QUERY_HEADS = 16
KEY_VALUE_HEADS = 8
WINDOW_LENGTH = 1024


rope_base = 10000.0
score_scale = 168.0 ** (-0.5)
norm_eps = 1e-06


def from_behind(value, axis, steps):
    count = lax.axis_size(axis)
    first, last = (max(0, -steps), min(count, count - steps))
    return lax.ppermute(value, axis, [(source, source + steps) for source in range(first, last)])


def rotary(field, positions):
    half = field.shape[-1] // 2
    freqs = rope_base ** (-jnp.arange(half, dtype=field.dtype) * 2.0 / field.shape[-1])
    angles = positions.astype(field.dtype)[:, None] * freqs[None, :]
    cosine = jnp.cos(angles)[:, None, :]
    sine = jnp.sin(angles)[:, None, :]
    first = field[..., :half]
    second = field[..., half:]
    return jnp.concatenate(
        [first * cosine - second * sine, second * cosine + first * sine], axis=-1
    )


def prepare(raw, gain, positions):
    meansq = jnp.mean(raw * raw, axis=-1, keepdims=True)
    normed = raw * lax.rsqrt(meansq + norm_eps) * gain
    return rotary(normed, positions)


def attend(query_blk, key_blk, value_blk, gradient_block, allowed):
    scores = (
        jnp.einsum("tgrd,wgd->grtw", query_blk, key_blk, preferred_element_type=jnp.float32)
        * score_scale
    )
    expd = jnp.where(allowed, jnp.exp(scores), 0.0)
    weights = expd / jnp.sum(expd, axis=-1, keepdims=True)
    weights_b = weights.astype(jnp.bfloat16)
    attention_probs = jnp.einsum(
        "grtw,wgd->tgrd", weights_b, value_blk, preferred_element_type=jnp.float32
    )
    delta_rows = jnp.einsum("jwkp,jwkp->wkj", gradient_block.astype(jnp.float32), attention_probs)
    dweights = jnp.einsum(
        "tgrd,wgd->grtw", gradient_block, value_blk, preferred_element_type=jnp.float32
    )
    dscores = (weights * (dweights - delta_rows[..., None])).astype(jnp.bfloat16)
    dquery = score_scale * jnp.einsum(
        "grtw,wgd->tgrd", dscores, key_blk, preferred_element_type=jnp.float32
    )
    dkey = score_scale * jnp.einsum(
        "grtw,tgrd->wgd", dscores, query_blk, preferred_element_type=jnp.float32
    )
    dvalue = jnp.einsum(
        "grtw,tgrd->wgd", weights_b, gradient_block, preferred_element_type=jnp.float32
    )
    return (dquery, dkey, dvalue)


def shards(query_proj, key_projection, value_proj, attn_grad, doc_ids, query_gain, key_norm_gain):
    row_count = query_proj.shape[1]
    behind = WINDOW_LENGTH // row_count
    group_ratio = QUERY_HEADS // KEY_VALUE_HEADS
    group_count = KEY_VALUE_HEADS // 2
    key_span_width = KEY_VALUE_HEADS * HEAD_SIZE
    base = lax.axis_index("seq") * row_count
    local = jnp.arange(row_count, dtype=jnp.int32)
    positions = base + local
    doc_row = doc_ids[0]

    def prepare_function(raw, gain):
        return prepare(raw, gain, positions)

    query_normalized, query_back = jax.vjp(
        prepare_function,
        query_proj[0].astype(jnp.float32).reshape(row_count, QUERY_HEADS, HEAD_SIZE),
        query_gain,
    )
    key_normalized, key_backward = jax.vjp(
        prepare_function,
        key_projection[0].astype(jnp.float32).reshape(row_count, KEY_VALUE_HEADS, HEAD_SIZE),
        key_norm_gain,
    )
    query_rot = query_normalized.astype(jnp.bfloat16)
    key_flat = key_normalized.astype(jnp.bfloat16).reshape(row_count, key_span_width)
    value_flat = value_proj[0]
    doc_rows = jnp.zeros((16, 2 * key_span_width), jnp.bfloat16)
    doc_rows = doc_rows.at[0, :row_count].set(doc_row.astype(jnp.bfloat16))
    packed = jnp.concatenate(
        [jnp.concatenate([key_flat, value_flat], axis=1), doc_rows], axis=0
    )
    parts = [from_behind(packed, "seq", offset) for offset in range(behind, 0, -1)]
    stacked = jnp.stack(parts + [packed])
    width = (behind + 1) * row_count
    key_win = stacked[:, :row_count, :key_span_width].reshape(width, key_span_width)
    value_win = stacked[:, :row_count, key_span_width:].reshape(width, key_span_width)
    key_doc = stacked[:, row_count, :row_count].reshape(width).astype(jnp.int32)
    key_pos = base - behind * row_count + jnp.arange(width, dtype=jnp.int32)
    allowed = (
        (key_pos[None, :] <= positions[:, None])
        & (positions[:, None] - key_pos[None, :] < WINDOW_LENGTH)
        & (key_pos[None, :] >= 0)
        & (key_doc[None, :] == doc_row[:, None])
    )
    query_groups = query_rot.reshape(row_count, group_count, 2, group_ratio, HEAD_SIZE).transpose(
        1, 0, 2, 3, 4
    )
    grad_groups = (
        attn_grad[0]
        .reshape(row_count, group_count, 2, group_ratio, HEAD_SIZE)
        .transpose(1, 0, 2, 3, 4)
    )
    key_groups = key_win.reshape(width, group_count, 2, HEAD_SIZE).transpose(1, 0, 2, 3)
    value_groups = value_win.reshape(width, group_count, 2, HEAD_SIZE).transpose(1, 0, 2, 3)

    def group_work(items):
        return attend(items[0], items[1], items[2], items[3], allowed)

    dquery_g, dkey_g, dvalue_g = lax.map(
        group_work, (query_groups, key_groups, value_groups, grad_groups)
    )
    dquery_rot = dquery_g.transpose(1, 0, 2, 3, 4).reshape(row_count, QUERY_HEADS, HEAD_SIZE)
    dkey_win = dkey_g.transpose(1, 0, 2, 3).reshape(behind + 1, row_count, key_span_width)
    dvalue_win = dvalue_g.transpose(1, 0, 2, 3).reshape(behind + 1, row_count, key_span_width)
    remote = jnp.concatenate([dkey_win[:behind], dvalue_win[:behind]], axis=2).astype(jnp.bfloat16)
    key_full_length = dkey_win[behind]
    value_total = dvalue_win[behind]
    for offset in range(1, behind + 1):
        moved = from_behind(remote[behind - offset], "seq", -offset).astype(jnp.float32)
        key_full_length = key_full_length + moved[:, :key_span_width]
        value_total = value_total + moved[:, key_span_width:]
    query_raw_gradient, query_gain_gradient = query_back(dquery_rot)
    key_raw_gradient, key_gain_gradient = key_backward(
        key_full_length.reshape(row_count, KEY_VALUE_HEADS, HEAD_SIZE)
    )
    gains = lax.psum((query_gain_gradient, key_gain_gradient), "dp")
    gain_query, gain_key = lax.psum(gains, "seq")
    return (
        query_raw_gradient.astype(jnp.bfloat16).reshape(1, row_count, QUERY_HEADS * HEAD_SIZE),
        key_raw_gradient.astype(jnp.bfloat16).reshape(1, row_count, key_span_width),
        value_total.astype(jnp.bfloat16)[None],
        gain_query,
        gain_key,
    )


def solution(mesh):
    in_specs = (
        P("dp", "seq", None),
        P("dp", "seq", None),
        P("dp", "seq", None),
        P("dp", "seq", None),
        P("dp", "seq"),
        P(),
        P(),
    )
    out_specs = (P("dp", "seq", None), P("dp", "seq", None), P("dp", "seq", None), P(), P())
    return jax.shard_map(shards, mesh=mesh, in_specs=in_specs, out_specs=out_specs, check_vma=False)
```

```python
import jax
import jax.numpy as jnp
from jax import lax
from jax.sharding import PartitionSpec as P

HEAD_SIZE = 128
QUERY_HEADS = 16
KEY_VALUE_HEADS = 8
WINDOW_LENGTH = 1024


rope_base = 10000.0
score_scale = 168.0 ** (-0.5)
norm_eps = 1e-06


SEQ_AXES = ("zh", "x", "y")
DP_AXES = ("zl", "c")


def from_behind(value, axis, steps):
    count = lax.axis_size(axis)
    first, last = (max(0, -steps), min(count, count - steps))
    return lax.ppermute(value, axis, [(source, source + steps) for source in range(first, last)])


def rotary(field, positions):
    half = field.shape[-1] // 2
    freqs = rope_base ** (-jnp.arange(half, dtype=field.dtype) * 2.0 / field.shape[-1])
    angles = positions.astype(field.dtype)[:, None] * freqs[None, :]
    cosine = jnp.cos(angles)[:, None, :]
    sine = jnp.sin(angles)[:, None, :]
    first = field[..., :half]
    second = field[..., half:]
    return jnp.concatenate(
        [first * cosine - second * sine, second * cosine + first * sine], axis=-1
    )


def prepare(raw, gain, positions):
    meansq = jnp.mean(raw * raw, axis=-1, keepdims=True)
    normed = raw * lax.rsqrt(meansq + norm_eps) * gain
    return rotary(normed, positions)


def attend(query_blk, key_blk, value_blk, gradient_block, allowed):
    scores = (
        jnp.einsum("tgrd,wgd->grtw", query_blk, key_blk, preferred_element_type=jnp.float32)
        * score_scale
    )
    expd = jnp.where(allowed, jnp.exp(scores), 0.0)
    weights = expd / jnp.sum(expd, axis=-1, keepdims=True)
    weights_b = weights.astype(jnp.bfloat16)
    attention_probs = jnp.einsum(
        "grtw,wgd->tgrd", weights_b, value_blk, preferred_element_type=jnp.float32
    )
    delta_rows = jnp.einsum("jwkp,jwkp->wkj", gradient_block.astype(jnp.float32), attention_probs)
    dweights = jnp.einsum(
        "tgrd,wgd->grtw", gradient_block, value_blk, preferred_element_type=jnp.float32
    )
    dscores = (weights * (dweights - delta_rows[..., None])).astype(jnp.bfloat16)
    dquery = score_scale * jnp.einsum(
        "grtw,wgd->tgrd", dscores, key_blk, preferred_element_type=jnp.float32
    )
    dkey = score_scale * jnp.einsum(
        "grtw,tgrd->wgd", dscores, query_blk, preferred_element_type=jnp.float32
    )
    dvalue = jnp.einsum(
        "grtw,tgrd->wgd", weights_b, gradient_block, preferred_element_type=jnp.float32
    )
    return (dquery, dkey, dvalue)


def shards(query_proj, key_projection, value_proj, attn_grad, doc_ids, query_gain, key_norm_gain):
    row_count = query_proj.shape[1]
    behind = WINDOW_LENGTH // row_count
    group_ratio = QUERY_HEADS // KEY_VALUE_HEADS
    group_count = KEY_VALUE_HEADS // 2
    key_span_width = KEY_VALUE_HEADS * HEAD_SIZE
    base = lax.axis_index(SEQ_AXES) * row_count
    local = jnp.arange(row_count, dtype=jnp.int32)
    positions = base + local
    doc_row = doc_ids[0]

    def prepare_function(raw, gain):
        return prepare(raw, gain, positions)

    query_normalized, query_back = jax.vjp(
        prepare_function,
        query_proj[0].astype(jnp.float32).reshape(row_count, QUERY_HEADS, HEAD_SIZE),
        query_gain,
    )
    key_normalized, key_backward = jax.vjp(
        prepare_function,
        key_projection[0].astype(jnp.float32).reshape(row_count, KEY_VALUE_HEADS, HEAD_SIZE),
        key_norm_gain,
    )
    query_rot = query_normalized.astype(jnp.bfloat16)
    key_flat = key_normalized.astype(jnp.bfloat16).reshape(row_count, key_span_width)
    value_flat = value_proj[0]
    doc_rows = jnp.zeros((16, 2 * key_span_width), jnp.bfloat16)
    doc_rows = doc_rows.at[0, :row_count].set(doc_row.astype(jnp.bfloat16))
    packed = jnp.concatenate(
        [jnp.concatenate([key_flat, value_flat], axis=1), doc_rows], axis=0
    )
    parts = [from_behind(packed, SEQ_AXES, offset) for offset in range(behind, 0, -1)]
    stacked = jnp.stack(parts + [packed])
    width = (behind + 1) * row_count
    key_win = stacked[:, :row_count, :key_span_width].reshape(width, key_span_width)
    value_win = stacked[:, :row_count, key_span_width:].reshape(width, key_span_width)
    key_doc = stacked[:, row_count, :row_count].reshape(width).astype(jnp.int32)
    key_pos = base - behind * row_count + jnp.arange(width, dtype=jnp.int32)
    allowed = (
        (key_pos[None, :] <= positions[:, None])
        & (positions[:, None] - key_pos[None, :] < WINDOW_LENGTH)
        & (key_pos[None, :] >= 0)
        & (key_doc[None, :] == doc_row[:, None])
    )
    query_groups = query_rot.reshape(row_count, group_count, 2, group_ratio, HEAD_SIZE).transpose(
        1, 0, 2, 3, 4
    )
    grad_groups = (
        attn_grad[0]
        .reshape(row_count, group_count, 2, group_ratio, HEAD_SIZE)
        .transpose(1, 0, 2, 3, 4)
    )
    key_groups = key_win.reshape(width, group_count, 2, HEAD_SIZE).transpose(1, 0, 2, 3)
    value_groups = value_win.reshape(width, group_count, 2, HEAD_SIZE).transpose(1, 0, 2, 3)

    def group_work(items):
        return attend(items[0], items[1], items[2], items[3], allowed)

    dquery_g, dkey_g, dvalue_g = lax.map(
        group_work, (query_groups, key_groups, value_groups, grad_groups)
    )
    dquery_rot = dquery_g.transpose(1, 0, 2, 3, 4).reshape(row_count, QUERY_HEADS, HEAD_SIZE)
    dkey_win = dkey_g.transpose(1, 0, 2, 3).reshape(behind + 1, row_count, key_span_width)
    dvalue_win = dvalue_g.transpose(1, 0, 2, 3).reshape(behind + 1, row_count, key_span_width)
    remote = jnp.concatenate([dkey_win[:behind], dvalue_win[:behind]], axis=2).astype(jnp.bfloat16)
    key_full_length = dkey_win[behind]
    value_total = dvalue_win[behind]
    for offset in range(1, behind + 1):
        moved = from_behind(remote[behind - offset], SEQ_AXES, -offset).astype(jnp.float32)
        key_full_length = key_full_length + moved[:, :key_span_width]
        value_total = value_total + moved[:, key_span_width:]
    query_raw_gradient, query_gain_gradient = query_back(dquery_rot)
    key_raw_gradient, key_gain_gradient = key_backward(
        key_full_length.reshape(row_count, KEY_VALUE_HEADS, HEAD_SIZE)
    )
    gains = (query_gain_gradient, key_gain_gradient)
    for axis in ("y", "x", "zh", "zl", "c"):
        gains = lax.psum(gains, axis)
    gain_query, gain_key = gains
    return (
        query_raw_gradient.astype(jnp.bfloat16).reshape(1, row_count, QUERY_HEADS * HEAD_SIZE),
        key_raw_gradient.astype(jnp.bfloat16).reshape(1, row_count, key_span_width),
        value_total.astype(jnp.bfloat16)[None],
        gain_query,
        gain_key,
    )


def solution(mesh):
    seq_size, dp_size = mesh.shape["seq"], mesh.shape["dp"]
    y_size = 8
    x_size = 4
    fine = jax.sharding.Mesh(
        mesh.devices.reshape(seq_size // (x_size * y_size), x_size, y_size, dp_size // 2, 2),
        ("zh", "x", "y", "zl", "c"),
    )
    tokens = P(DP_AXES, SEQ_AXES, None)
    in_specs = (tokens, tokens, tokens, tokens, P(DP_AXES, SEQ_AXES), P(), P())
    out_specs = (tokens, tokens, tokens, P(), P())
    return jax.shard_map(shards, mesh=fine, in_specs=in_specs, out_specs=out_specs, check_vma=False)
```

```python
import jax
import jax.numpy as jnp
from jax import lax
from jax.sharding import PartitionSpec as P

HEAD_SIZE = 128
QUERY_HEADS = 16
KEY_VALUE_HEADS = 8
WINDOW_LENGTH = 1024


rope_base = 10000.0
score_scale = 168.0 ** (-0.5)
norm_eps = 1e-06


SEQ_AXES = ("zh", "x", "y")
DP_AXES = ("zl", "c")


def from_behind(value, axis, steps):
    count = lax.axis_size(axis)
    first, last = (max(0, -steps), min(count, count - steps))
    return lax.ppermute(value, axis, [(source, source + steps) for source in range(first, last)])


def rotary(field, positions):
    half = field.shape[-1] // 2
    freqs = rope_base ** (-jnp.arange(half, dtype=field.dtype) * 2.0 / field.shape[-1])
    angles = positions.astype(field.dtype)[:, None] * freqs[None, :]
    cosine = jnp.cos(angles)[:, None, :]
    sine = jnp.sin(angles)[:, None, :]
    first = field[..., :half]
    second = field[..., half:]
    return jnp.concatenate(
        [first * cosine - second * sine, second * cosine + first * sine], axis=-1
    )


def prepare(raw, gain, positions):
    meansq = jnp.mean(raw * raw, axis=-1, keepdims=True)
    normed = raw * lax.rsqrt(meansq + norm_eps) * gain
    return rotary(normed, positions)


def attend(query_blk, key_blk, value_blk, gradient_block, allowed):
    scores = (
        jnp.einsum("tgrd,wgd->grtw", query_blk, key_blk, preferred_element_type=jnp.float32)
        * score_scale
    )
    expd = jnp.where(allowed, jnp.exp(scores), 0.0)
    weights = expd / jnp.sum(expd, axis=-1, keepdims=True)
    weights_b = weights.astype(jnp.bfloat16)
    attention_probs = jnp.einsum(
        "grtw,wgd->tgrd", weights_b, value_blk, preferred_element_type=jnp.float32
    )
    delta_rows = jnp.einsum("jwkp,jwkp->wkj", gradient_block.astype(jnp.float32), attention_probs)
    dweights = jnp.einsum(
        "tgrd,wgd->grtw", gradient_block, value_blk, preferred_element_type=jnp.float32
    )
    dscores = (weights * (dweights - delta_rows[..., None])).astype(jnp.bfloat16)
    dquery = score_scale * jnp.einsum(
        "grtw,wgd->tgrd", dscores, key_blk, preferred_element_type=jnp.float32
    )
    dkey = score_scale * jnp.einsum(
        "grtw,tgrd->wgd", dscores, query_blk, preferred_element_type=jnp.float32
    )
    dvalue = jnp.einsum(
        "grtw,tgrd->wgd", weights_b, gradient_block, preferred_element_type=jnp.float32
    )
    return (dquery, dkey, dvalue)


def shards(query_proj, key_projection, value_proj, attn_grad, doc_ids, query_gain, key_norm_gain):
    row_count = query_proj.shape[1]
    behind = WINDOW_LENGTH // row_count
    group_ratio = QUERY_HEADS // KEY_VALUE_HEADS
    group_count = KEY_VALUE_HEADS // 2
    key_span_width = KEY_VALUE_HEADS * HEAD_SIZE
    base = lax.axis_index(SEQ_AXES) * row_count
    local = jnp.arange(row_count, dtype=jnp.int32)
    positions = base + local
    doc_row = doc_ids[0]

    def prepare_function(raw, gain):
        return prepare(raw, gain, positions)

    query_normalized, query_back = jax.vjp(
        prepare_function,
        query_proj[0].astype(jnp.float32).reshape(row_count, QUERY_HEADS, HEAD_SIZE),
        query_gain,
    )
    query_rot = query_normalized.astype(jnp.bfloat16)
    value_flat = value_proj[0]
    doc_rows = jnp.zeros((16, 2 * key_span_width), jnp.bfloat16)
    doc_rows = doc_rows.at[0, :row_count].set(doc_row.astype(jnp.bfloat16))
    packed = jnp.concatenate(
        [jnp.concatenate([key_projection[0], value_flat], axis=1), doc_rows], axis=0
    )
    parts = [from_behind(packed, SEQ_AXES, offset) for offset in range(behind, 0, -1)]
    stacked = jnp.stack(parts + [packed])
    width = (behind + 1) * row_count
    key_raw_win = stacked[:, :row_count, :key_span_width].reshape(width, KEY_VALUE_HEADS, HEAD_SIZE)
    value_win = stacked[:, :row_count, key_span_width:].reshape(width, KEY_VALUE_HEADS, HEAD_SIZE)
    key_doc = stacked[:, row_count, :row_count].reshape(width).astype(jnp.int32)
    key_pos = base - behind * row_count + jnp.arange(width, dtype=jnp.int32)

    def prepare_window(raw, gain):
        return prepare(raw, gain, key_pos)

    key_normalized_win, key_window_back = jax.vjp(
        prepare_window, key_raw_win.astype(jnp.float32), key_norm_gain
    )
    key_win = key_normalized_win.astype(jnp.bfloat16)
    allowed = (
        (key_pos[None, :] <= positions[:, None])
        & (positions[:, None] - key_pos[None, :] < WINDOW_LENGTH)
        & (key_pos[None, :] >= 0)
        & (key_doc[None, :] == doc_row[:, None])
    )
    dquery_rot, dkey_win, dvalue_win = attend(
        query_rot.reshape(row_count, KEY_VALUE_HEADS, group_ratio, HEAD_SIZE),
        key_win,
        value_win,
        attn_grad[0].reshape(row_count, KEY_VALUE_HEADS, group_ratio, HEAD_SIZE),
        allowed,
    )
    dquery_rot = dquery_rot.reshape(row_count, QUERY_HEADS, HEAD_SIZE)
    dkey_win = dkey_win.reshape(behind + 1, row_count, key_span_width)
    dvalue_win = dvalue_win.reshape(behind + 1, row_count, key_span_width)
    remote_key = dkey_win[:behind].astype(jnp.bfloat16)
    remote = jnp.concatenate([remote_key, dvalue_win[:behind].astype(jnp.bfloat16)], axis=2)
    owned = jnp.concatenate([remote_key.astype(jnp.float32), dkey_win[behind:]], axis=0)
    _, key_gain_gradient = key_window_back(owned.reshape(width, KEY_VALUE_HEADS, HEAD_SIZE))
    query_raw_gradient, query_gain_gradient = query_back(dquery_rot)
    sent = [from_behind(remote[behind - offset], SEQ_AXES, -offset) for offset in range(1, behind + 1)]
    gains = (query_gain_gradient, key_gain_gradient)
    for axis in ("y", "x", "zh", "zl", "c"):
        gains = lax.psum(gains, axis)
    gain_query, gain_key = gains
    key_full_length = dkey_win[behind]
    value_total = dvalue_win[behind]
    for moved in sent:
        moved = moved.astype(jnp.float32)
        key_full_length = key_full_length + moved[:, :key_span_width]
        value_total = value_total + moved[:, key_span_width:]
    _, key_backward = jax.vjp(
        prepare_function,
        key_projection[0].astype(jnp.float32).reshape(row_count, KEY_VALUE_HEADS, HEAD_SIZE),
        key_norm_gain,
    )
    key_raw_gradient, _ = key_backward(
        key_full_length.reshape(row_count, KEY_VALUE_HEADS, HEAD_SIZE)
    )
    return (
        query_raw_gradient.astype(jnp.bfloat16).reshape(1, row_count, QUERY_HEADS * HEAD_SIZE),
        key_raw_gradient.astype(jnp.bfloat16).reshape(1, row_count, key_span_width),
        value_total.astype(jnp.bfloat16)[None],
        gain_query,
        gain_key,
    )


def solution(mesh):
    seq_size, dp_size = mesh.shape["seq"], mesh.shape["dp"]
    y_size = 8
    x_size = 4
    fine = jax.sharding.Mesh(
        mesh.devices.reshape(seq_size // (x_size * y_size), x_size, y_size, dp_size // 2, 2),
        ("zh", "x", "y", "zl", "c"),
    )
    tokens = P(DP_AXES, SEQ_AXES, None)
    in_specs = (tokens, tokens, tokens, tokens, P(DP_AXES, SEQ_AXES), P(), P())
    out_specs = (tokens, tokens, tokens, P(), P())
    return jax.shard_map(shards, mesh=fine, in_specs=in_specs, out_specs=out_specs, check_vma=False)
```

```python
import jax
import jax.numpy as jnp
from jax import lax
from jax.sharding import PartitionSpec as P

HEAD_SIZE = 128
QUERY_HEADS = 16
KEY_VALUE_HEADS = 8
WINDOW_LENGTH = 1024


rope_base = 10000.0
score_scale = 168.0 ** (-0.5)
norm_eps = 1e-06


SEQ_AXES = ("zh", "x", "y")
DP_AXES = ("zl", "c")


def shift(value, steps, cyclic):
    count = lax.axis_size(SEQ_AXES)
    if cyclic:
        pairs = [(source, (source + steps) % count) for source in range(count)]
    else:
        pairs = [(source, source + steps) for source in range(max(0, -steps), min(count, count - steps))]
    return lax.ppermute(value, SEQ_AXES, pairs)


def rotary(field, positions):
    half = field.shape[-1] // 2
    freqs = rope_base ** (-jnp.arange(half, dtype=field.dtype) * 2.0 / field.shape[-1])
    angles = positions.astype(field.dtype)[:, None] * freqs[None, :]
    cosine = jnp.cos(angles)[:, None, :]
    sine = jnp.sin(angles)[:, None, :]
    first = field[..., :half]
    second = field[..., half:]
    return jnp.concatenate(
        [first * cosine - second * sine, second * cosine + first * sine], axis=-1
    )


def prepare(raw, gain, positions):
    meansq = jnp.mean(raw * raw, axis=-1, keepdims=True)
    normed = raw * lax.rsqrt(meansq + norm_eps) * gain
    return rotary(normed, positions)


def attend(query_blk, key_blk, value_blk, gradient_block, allowed):
    scores = (
        jnp.einsum("tgrd,wgd->grtw", query_blk, key_blk, preferred_element_type=jnp.float32)
        * score_scale
    )
    expd = jnp.where(allowed, jnp.exp(scores), 0.0)
    weights = expd / jnp.sum(expd, axis=-1, keepdims=True)
    weights_b = weights.astype(jnp.bfloat16)
    attention_probs = jnp.einsum(
        "grtw,wgd->tgrd", weights_b, value_blk, preferred_element_type=jnp.float32
    )
    delta_rows = jnp.einsum("jwkp,jwkp->wkj", gradient_block.astype(jnp.float32), attention_probs)
    dweights = jnp.einsum(
        "tgrd,wgd->grtw", gradient_block, value_blk, preferred_element_type=jnp.float32
    )
    dscores = (weights * (dweights - delta_rows[..., None])).astype(jnp.bfloat16)
    dquery = score_scale * jnp.einsum(
        "grtw,wgd->tgrd", dscores, key_blk, preferred_element_type=jnp.float32
    )
    dkey = score_scale * jnp.einsum(
        "grtw,tgrd->wgd", dscores, query_blk, preferred_element_type=jnp.float32
    )
    dvalue = jnp.einsum(
        "grtw,tgrd->wgd", weights_b, gradient_block, preferred_element_type=jnp.float32
    )
    return (dquery, dkey, dvalue)


def shards(query_proj, key_projection, value_proj, attn_grad, doc_ids, query_gain, key_norm_gain):
    row_count = query_proj.shape[1]
    behind = WINDOW_LENGTH // row_count
    group_ratio = QUERY_HEADS // KEY_VALUE_HEADS
    group_count = KEY_VALUE_HEADS // 2
    key_span_width = KEY_VALUE_HEADS * HEAD_SIZE
    base = lax.axis_index(SEQ_AXES) * row_count
    local = jnp.arange(row_count, dtype=jnp.int32)
    positions = base + local
    doc_row = doc_ids[0]

    def prepare_function(raw, gain):
        return prepare(raw, gain, positions)

    query_normalized, query_back = jax.vjp(
        prepare_function,
        query_proj[0].astype(jnp.float32).reshape(row_count, QUERY_HEADS, HEAD_SIZE),
        query_gain,
    )
    query_rot = query_normalized.astype(jnp.bfloat16)
    value_flat = value_proj[0]
    doc_rows = jnp.zeros((16, 2 * key_span_width), jnp.bfloat16)
    doc_rows = doc_rows.at[0, :row_count].set(doc_row.astype(jnp.bfloat16))
    packed = jnp.concatenate(
        [jnp.concatenate([key_projection[0], value_flat], axis=1), doc_rows], axis=0
    )
    half = behind // 2
    near, far = [], []
    a_slot, b_slot = packed, packed
    for step in range(half):
        a_slot = shift(a_slot, 1, False)
        b_slot = shift(b_slot, behind if step == 0 else -1, True)
        near.append(a_slot)
        far.append(b_slot)
    stacked = jnp.stack(far + near[::-1] + [packed])
    width = (behind + 1) * row_count
    key_raw_win = stacked[:, :row_count, :key_span_width].reshape(width, KEY_VALUE_HEADS, HEAD_SIZE)
    value_win = stacked[:, :row_count, key_span_width:].reshape(width, KEY_VALUE_HEADS, HEAD_SIZE)
    key_doc = stacked[:, row_count, :row_count].reshape(width).astype(jnp.int32)
    key_pos = base - behind * row_count + jnp.arange(width, dtype=jnp.int32)

    def prepare_window(raw, gain):
        return prepare(raw, gain, key_pos)

    key_normalized_win, key_window_back = jax.vjp(
        prepare_window, key_raw_win.astype(jnp.float32), key_norm_gain
    )
    key_win = key_normalized_win.astype(jnp.bfloat16)
    allowed = (
        (key_pos[None, :] <= positions[:, None])
        & (positions[:, None] - key_pos[None, :] < WINDOW_LENGTH)
        & (key_pos[None, :] >= 0)
        & (key_doc[None, :] == doc_row[:, None])
    )
    dquery_rot, dkey_win, dvalue_win = attend(
        query_rot.reshape(row_count, KEY_VALUE_HEADS, group_ratio, HEAD_SIZE),
        key_win,
        value_win,
        attn_grad[0].reshape(row_count, KEY_VALUE_HEADS, group_ratio, HEAD_SIZE),
        allowed,
    )
    dquery_rot = dquery_rot.reshape(row_count, QUERY_HEADS, HEAD_SIZE)
    dkey_win = dkey_win.reshape(behind + 1, row_count, key_span_width)
    dvalue_win = dvalue_win.reshape(behind + 1, row_count, key_span_width)
    remote_key = dkey_win[:behind].astype(jnp.bfloat16)
    remote_f32 = jnp.concatenate([dkey_win[:behind], dvalue_win[:behind]], axis=2)
    remote = remote_f32.astype(jnp.bfloat16)
    owned = jnp.concatenate([remote_key.astype(jnp.float32), dkey_win[behind:]], axis=0)
    _, key_gain_gradient = key_window_back(owned.reshape(width, KEY_VALUE_HEADS, HEAD_SIZE))
    query_raw_gradient, query_gain_gradient = query_back(dquery_rot)
    carry_near = remote[behind - half]
    for offset in range(half - 1, 0, -1):
        got = shift(carry_near, -1, False).astype(jnp.float32)
        carry_near = (got + remote_f32[behind - offset]).astype(jnp.bfloat16)
    carry_far = remote[behind - half - 1]
    for offset in range(half + 2, behind + 1):
        got = shift(carry_far, 1, True).astype(jnp.float32)
        carry_far = (got + remote_f32[behind - offset]).astype(jnp.bfloat16)
    sent = [shift(carry_near, -1, False), shift(carry_far, -behind, True)]
    gains = (query_gain_gradient, key_gain_gradient)
    for axis in ("y", "x", "zh", "zl", "c"):
        gains = lax.psum(gains, axis)
    gain_query, gain_key = gains
    key_full_length = dkey_win[behind]
    value_total = dvalue_win[behind]
    for moved in sent:
        moved = moved.astype(jnp.float32)
        key_full_length = key_full_length + moved[:, :key_span_width]
        value_total = value_total + moved[:, key_span_width:]
    _, key_backward = jax.vjp(
        prepare_function,
        key_projection[0].astype(jnp.float32).reshape(row_count, KEY_VALUE_HEADS, HEAD_SIZE),
        key_norm_gain,
    )
    key_raw_gradient, _ = key_backward(
        key_full_length.reshape(row_count, KEY_VALUE_HEADS, HEAD_SIZE)
    )
    return (
        query_raw_gradient.astype(jnp.bfloat16).reshape(1, row_count, QUERY_HEADS * HEAD_SIZE),
        key_raw_gradient.astype(jnp.bfloat16).reshape(1, row_count, key_span_width),
        value_total.astype(jnp.bfloat16)[None],
        gain_query,
        gain_key,
    )


def solution(mesh):
    seq_size, dp_size = mesh.shape["seq"], mesh.shape["dp"]
    y_size = 8
    x_size = 4
    fine = jax.sharding.Mesh(
        mesh.devices.reshape(seq_size // (x_size * y_size), x_size, y_size, dp_size // 2, 2),
        ("zh", "x", "y", "zl", "c"),
    )
    tokens = P(DP_AXES, SEQ_AXES, None)
    in_specs = (tokens, tokens, tokens, tokens, P(DP_AXES, SEQ_AXES), P(), P())
    out_specs = (tokens, tokens, tokens, P(), P())
    return jax.shard_map(shards, mesh=fine, in_specs=in_specs, out_specs=out_specs, check_vma=False)
```

```python
import jax
import jax.numpy as jnp
from jax import lax
from jax.sharding import PartitionSpec as P

HEAD_SIZE = 128
QUERY_HEADS = 16
KEY_VALUE_HEADS = 8
WINDOW_LENGTH = 1024


rope_base = 10000.0
score_scale = 168.0 ** (-0.5)
norm_eps = 1e-06


SEQ_AXES = ("zh", "x", "y")
DP_AXES = ("zl", "c")


def shift(value, steps, cyclic):
    count = lax.axis_size(SEQ_AXES)
    if cyclic:
        pairs = [(source, (source + steps) % count) for source in range(count)]
    else:
        pairs = [(source, source + steps) for source in range(max(0, -steps), min(count, count - steps))]
    return lax.ppermute(value, SEQ_AXES, pairs)


def rotary(field, positions):
    half = field.shape[-1] // 2
    freqs = rope_base ** (-jnp.arange(half, dtype=field.dtype) * 2.0 / field.shape[-1])
    angles = positions.astype(field.dtype)[:, None] * freqs[None, :]
    cosine = jnp.cos(angles)[:, None, :]
    sine = jnp.sin(angles)[:, None, :]
    first = field[..., :half]
    second = field[..., half:]
    return jnp.concatenate(
        [first * cosine - second * sine, second * cosine + first * sine], axis=-1
    )


def prepare(raw, gain, positions):
    meansq = jnp.mean(raw * raw, axis=-1, keepdims=True)
    normed = raw * lax.rsqrt(meansq + norm_eps) * gain
    return rotary(normed, positions)


def attend(query_blk, key_blk, value_blk, gradient_block, allowed):
    scores = (
        jnp.einsum("tgrd,wgd->grtw", query_blk, key_blk, preferred_element_type=jnp.float32)
        * score_scale
    )
    expd = jnp.where(allowed, jnp.exp(scores), 0.0)
    weights = expd / jnp.sum(expd, axis=-1, keepdims=True)
    weights_b = weights.astype(jnp.bfloat16)
    attention_probs = jnp.einsum(
        "grtw,wgd->tgrd", weights_b, value_blk, preferred_element_type=jnp.float32
    )
    delta_rows = jnp.einsum("jwkp,jwkp->wkj", gradient_block.astype(jnp.float32), attention_probs)
    dweights = jnp.einsum(
        "tgrd,wgd->grtw", gradient_block, value_blk, preferred_element_type=jnp.float32
    )
    dscores = (weights * (dweights - delta_rows[..., None])).astype(jnp.bfloat16)
    dquery = score_scale * jnp.einsum(
        "grtw,wgd->tgrd", dscores, key_blk, preferred_element_type=jnp.float32
    )
    dkey = score_scale * jnp.einsum(
        "grtw,tgrd->gwd", dscores, query_blk, preferred_element_type=jnp.float32
    )
    dvalue = jnp.einsum(
        "grtw,tgrd->gwd", weights_b, gradient_block, preferred_element_type=jnp.float32
    )
    return (dquery, dkey, dvalue)


def shards(query_proj, key_projection, value_proj, attn_grad, doc_ids, query_gain, key_norm_gain):
    row_count = query_proj.shape[1]
    behind = WINDOW_LENGTH // row_count
    group_ratio = QUERY_HEADS // KEY_VALUE_HEADS
    group_count = KEY_VALUE_HEADS // 2
    key_span_width = KEY_VALUE_HEADS * HEAD_SIZE
    base = lax.axis_index(SEQ_AXES) * row_count
    local = jnp.arange(row_count, dtype=jnp.int32)
    positions = base + local
    doc_row = doc_ids[0]

    def prepare_function(raw, gain):
        return prepare(raw, gain, positions)

    query_normalized, query_back = jax.vjp(
        prepare_function,
        query_proj[0].astype(jnp.float32).reshape(row_count, QUERY_HEADS, HEAD_SIZE),
        query_gain,
    )
    query_rot = query_normalized.astype(jnp.bfloat16)
    value_flat = value_proj[0]
    doc_rows = jnp.zeros((16, 2 * key_span_width), jnp.bfloat16)
    doc_rows = doc_rows.at[0, :row_count].set(doc_row.astype(jnp.bfloat16))
    packed = jnp.concatenate(
        [jnp.concatenate([key_projection[0], value_flat], axis=1), doc_rows], axis=0
    )
    half = behind // 2
    near, far = [], []
    a_slot, b_slot = packed, packed
    for step in range(half):
        a_slot = shift(a_slot, 1, False)
        b_slot = shift(b_slot, behind if step == 0 else -1, True)
        near.append(a_slot)
        far.append(b_slot)
    stacked = jnp.stack(far + near[::-1] + [packed])
    width = (behind + 1) * row_count
    key_raw_win = stacked[:, :row_count, :key_span_width].reshape(width, KEY_VALUE_HEADS, HEAD_SIZE)
    value_win = stacked[:, :row_count, key_span_width:].reshape(width, KEY_VALUE_HEADS, HEAD_SIZE)
    key_doc = stacked[:, row_count, :row_count].reshape(width).astype(jnp.int32)
    key_pos = base - behind * row_count + jnp.arange(width, dtype=jnp.int32)

    def prepare_window(raw, gain):
        return prepare(raw, gain, key_pos)

    key_normalized_win, key_window_back = jax.vjp(
        prepare_window, key_raw_win.astype(jnp.float32), key_norm_gain
    )
    key_win = key_normalized_win.astype(jnp.bfloat16)
    allowed = (
        (key_pos[None, :] <= positions[:, None])
        & (positions[:, None] - key_pos[None, :] < WINDOW_LENGTH)
        & (key_pos[None, :] >= 0)
        & (key_doc[None, :] == doc_row[:, None])
    )
    dquery_rot, dkey_win, dvalue_win = attend(
        query_rot.reshape(row_count, KEY_VALUE_HEADS, group_ratio, HEAD_SIZE),
        key_win,
        value_win,
        attn_grad[0].reshape(row_count, KEY_VALUE_HEADS, group_ratio, HEAD_SIZE),
        allowed,
    )
    dquery_rot = dquery_rot.reshape(row_count, QUERY_HEADS, HEAD_SIZE)
    slots = jnp.stack([dkey_win, dvalue_win]).reshape(
        2, KEY_VALUE_HEADS, behind + 1, row_count, HEAD_SIZE
    )
    remote = slots[:, :, :behind].astype(jnp.bfloat16)
    owned = jnp.concatenate(
        [remote[0].astype(jnp.float32), slots[0, :, behind:]], axis=1
    ).reshape(KEY_VALUE_HEADS, width, HEAD_SIZE)
    _, key_gain_gradient = key_window_back(owned.transpose(1, 0, 2))
    query_raw_gradient, query_gain_gradient = query_back(dquery_rot)
    carry_near = remote[:, :, behind - half]
    for offset in range(half - 1, 0, -1):
        got = shift(carry_near, -1, False).astype(jnp.float32)
        carry_near = (got + slots[:, :, behind - offset]).astype(jnp.bfloat16)
    carry_far = remote[:, :, behind - half - 1]
    for offset in range(half + 2, behind + 1):
        got = shift(carry_far, 1, True).astype(jnp.float32)
        carry_far = (got + slots[:, :, behind - offset]).astype(jnp.bfloat16)
    sent = [shift(carry_near, -1, False), shift(carry_far, -behind, True)]
    gains = (query_gain_gradient, key_gain_gradient)
    for axis in ("y", "x", "zh", "zl", "c"):
        gains = lax.psum(gains, axis)
    gain_query, gain_key = gains
    total = slots[:, :, behind]
    for moved in sent:
        total = total + moved.astype(jnp.float32)
    key_full_length = total[0].transpose(1, 0, 2).reshape(row_count, key_span_width)
    value_total = total[1].transpose(1, 0, 2).reshape(row_count, key_span_width)
    _, key_backward = jax.vjp(
        prepare_function,
        key_projection[0].astype(jnp.float32).reshape(row_count, KEY_VALUE_HEADS, HEAD_SIZE),
        key_norm_gain,
    )
    key_raw_gradient, _ = key_backward(
        key_full_length.reshape(row_count, KEY_VALUE_HEADS, HEAD_SIZE)
    )
    return (
        query_raw_gradient.astype(jnp.bfloat16).reshape(1, row_count, QUERY_HEADS * HEAD_SIZE),
        key_raw_gradient.astype(jnp.bfloat16).reshape(1, row_count, key_span_width),
        value_total.astype(jnp.bfloat16)[None],
        gain_query,
        gain_key,
    )


def solution(mesh):
    seq_size, dp_size = mesh.shape["seq"], mesh.shape["dp"]
    y_size = 8
    x_size = 4
    fine = jax.sharding.Mesh(
        mesh.devices.reshape(seq_size // (x_size * y_size), x_size, y_size, dp_size // 2, 2),
        ("zh", "x", "y", "zl", "c"),
    )
    tokens = P(DP_AXES, SEQ_AXES, None)
    in_specs = (tokens, tokens, tokens, tokens, P(DP_AXES, SEQ_AXES), P(), P())
    out_specs = (tokens, tokens, tokens, P(), P())
    return jax.shard_map(shards, mesh=fine, in_specs=in_specs, out_specs=out_specs, check_vma=False)
```

```python
import jax
import jax.numpy as jnp
from jax import lax
from jax.sharding import PartitionSpec as P

HEAD_SIZE = 128
QUERY_HEADS = 16
KEY_VALUE_HEADS = 8
WINDOW_LENGTH = 1024


rope_base = 10000.0
score_scale = 168.0 ** (-0.5)
norm_eps = 1e-06


SEQ_AXES = ("zh", "x", "y")
DP_AXES = ("zl", "c")


def shift(value, steps, cyclic):
    count = lax.axis_size(SEQ_AXES)
    if cyclic:
        pairs = [(source, (source + steps) % count) for source in range(count)]
    else:
        pairs = [(source, source + steps) for source in range(max(0, -steps), min(count, count - steps))]
    return lax.ppermute(value, SEQ_AXES, pairs)


def rotary(field, positions):
    half = field.shape[-1] // 2
    freqs = rope_base ** (-jnp.arange(half, dtype=field.dtype) * 2.0 / field.shape[-1])
    angles = positions.astype(field.dtype)[:, None] * freqs[None, :]
    cosine = jnp.cos(angles)[:, None, :]
    sine = jnp.sin(angles)[:, None, :]
    first = field[..., :half]
    second = field[..., half:]
    return jnp.concatenate(
        [first * cosine - second * sine, second * cosine + first * sine], axis=-1
    )


def prepare(raw, gain, positions):
    meansq = jnp.mean(raw * raw, axis=-1, keepdims=True)
    normed = raw * lax.rsqrt(meansq + norm_eps) * gain
    return rotary(normed, positions)


def attend(query_blk, key_blk, value_blk, gradient_block, allowed):
    scores = (
        jnp.einsum("tgrd,wgd->grtw", query_blk, key_blk, preferred_element_type=jnp.float32)
        * score_scale
    )
    expd = jnp.where(allowed, jnp.exp(scores), 0.0)
    weights = expd / jnp.sum(expd, axis=-1, keepdims=True)
    weights_b = weights.astype(jnp.bfloat16)
    attention_probs = jnp.einsum(
        "grtw,wgd->tgrd", weights_b, value_blk, preferred_element_type=jnp.float32
    )
    delta_rows = jnp.einsum("jwkp,jwkp->wkj", gradient_block.astype(jnp.float32), attention_probs)
    dweights = jnp.einsum(
        "tgrd,wgd->grtw", gradient_block, value_blk, preferred_element_type=jnp.float32
    )
    dscores = (weights * (dweights - delta_rows[..., None])).astype(jnp.bfloat16)
    dquery = score_scale * jnp.einsum(
        "grtw,wgd->tgrd", dscores, key_blk, preferred_element_type=jnp.float32
    )
    dkey = score_scale * jnp.einsum(
        "grtw,tgrd->gwd", dscores, query_blk, preferred_element_type=jnp.float32
    )
    dvalue = jnp.einsum(
        "grtw,tgrd->gwd", weights_b, gradient_block, preferred_element_type=jnp.float32
    )
    return (dquery, dkey, dvalue)


def shards(query_proj, key_projection, value_proj, attn_grad, doc_ids, query_gain, key_norm_gain):
    row_count = query_proj.shape[1]
    behind = WINDOW_LENGTH // row_count
    group_ratio = QUERY_HEADS // KEY_VALUE_HEADS
    group_count = KEY_VALUE_HEADS // 2
    key_span_width = KEY_VALUE_HEADS * HEAD_SIZE
    base = lax.axis_index(SEQ_AXES) * row_count
    local = jnp.arange(row_count, dtype=jnp.int32)
    positions = base + local
    doc_row = doc_ids[0]

    def prepare_function(raw, gain):
        return prepare(raw, gain, positions)

    query_normalized, query_back = jax.vjp(
        prepare_function,
        query_proj[0].astype(jnp.float32).reshape(row_count, QUERY_HEADS, HEAD_SIZE),
        query_gain,
    )
    query_rot = query_normalized.astype(jnp.bfloat16)
    value_flat = value_proj[0]
    doc_rows = jnp.zeros((16, 2 * key_span_width), jnp.bfloat16)
    doc_rows = doc_rows.at[0, :row_count].set(doc_row.astype(jnp.bfloat16))
    packed = jnp.concatenate(
        [jnp.concatenate([key_projection[0], value_flat], axis=1), doc_rows], axis=0
    )
    half = behind // 2
    near, far = [], []
    a_slot, b_slot = packed, packed
    for step in range(half):
        a_slot = shift(a_slot, 1, False)
        b_slot = shift(b_slot, behind if step == 0 else -1, True)
        near.append(a_slot)
        far.append(b_slot)
    stacked = jnp.stack(far + near[::-1] + [packed])
    width = (behind + 1) * row_count
    key_raw_win = stacked[:, :row_count, :key_span_width].reshape(width, KEY_VALUE_HEADS, HEAD_SIZE)
    value_win = stacked[:, :row_count, key_span_width:].reshape(width, KEY_VALUE_HEADS, HEAD_SIZE)
    key_doc = stacked[:, row_count, :row_count].reshape(width).astype(jnp.int32)
    key_pos = base - behind * row_count + jnp.arange(width, dtype=jnp.int32)

    def prepare_window(raw, gain):
        return prepare(raw, gain, key_pos)

    key_normalized_win, key_window_back = jax.vjp(
        prepare_window, key_raw_win.astype(jnp.float32), key_norm_gain
    )
    key_win = key_normalized_win.astype(jnp.bfloat16)
    allowed = (
        (key_pos[None, :] <= positions[:, None])
        & (positions[:, None] - key_pos[None, :] < WINDOW_LENGTH)
        & (key_pos[None, :] >= 0)
        & (key_doc[None, :] == doc_row[:, None])
    )
    dquery_rot, dkey_win, dvalue_win = attend(
        query_rot.reshape(row_count, KEY_VALUE_HEADS, group_ratio, HEAD_SIZE),
        key_win,
        value_win,
        attn_grad[0].reshape(row_count, KEY_VALUE_HEADS, group_ratio, HEAD_SIZE),
        allowed,
    )
    dquery_rot = dquery_rot.reshape(row_count, QUERY_HEADS, HEAD_SIZE)
    slots = jnp.stack([dkey_win, dvalue_win]).reshape(
        2, KEY_VALUE_HEADS, behind + 1, row_count, HEAD_SIZE
    )
    remote = slots[:, :, :behind].astype(jnp.bfloat16)
    owned = jnp.concatenate(
        [remote[0].astype(jnp.float32), slots[0, :, behind:]], axis=1
    ).reshape(KEY_VALUE_HEADS, width, HEAD_SIZE)
    _, key_gain_gradient = key_window_back(owned.transpose(1, 0, 2))
    query_raw_gradient, query_gain_gradient = query_back(dquery_rot)
    carry_near = remote[:, :, behind - half]
    for offset in range(half - 1, 0, -1):
        got = shift(carry_near, -1, False).astype(jnp.float32)
        carry_near = (got + slots[:, :, behind - offset]).astype(jnp.bfloat16)
    carry_far = remote[:, :, behind - half - 1]
    for offset in range(half + 2, behind + 1):
        got = shift(carry_far, 1, True).astype(jnp.float32)
        carry_far = (got + slots[:, :, behind - offset]).astype(jnp.bfloat16)
    gains, carry_near, carry_far = lax.optimization_barrier(
        ((query_gain_gradient, key_gain_gradient), carry_near, carry_far)
    )
    sent = [shift(carry_near, -1, False), shift(carry_far, -behind, True)]
    for axis in ("y", "x", "zh", "zl", "c"):
        gains = lax.psum(gains, axis)
    gains, total = lax.optimization_barrier((gains, slots[:, :, behind]))
    gain_query, gain_key = gains
    for moved in sent:
        total = total + moved.astype(jnp.float32)
    key_full_length = total[0].transpose(1, 0, 2).reshape(row_count, key_span_width)
    value_total = total[1].transpose(1, 0, 2).reshape(row_count, key_span_width)
    _, key_backward = jax.vjp(
        prepare_function,
        key_projection[0].astype(jnp.float32).reshape(row_count, KEY_VALUE_HEADS, HEAD_SIZE),
        key_norm_gain,
    )
    key_raw_gradient, _ = key_backward(
        key_full_length.reshape(row_count, KEY_VALUE_HEADS, HEAD_SIZE)
    )
    return (
        query_raw_gradient.astype(jnp.bfloat16).reshape(1, row_count, QUERY_HEADS * HEAD_SIZE),
        key_raw_gradient.astype(jnp.bfloat16).reshape(1, row_count, key_span_width),
        value_total.astype(jnp.bfloat16)[None],
        gain_query,
        gain_key,
    )


def solution(mesh):
    seq_size, dp_size = mesh.shape["seq"], mesh.shape["dp"]
    y_size = 8
    x_size = 4
    fine = jax.sharding.Mesh(
        mesh.devices.reshape(seq_size // (x_size * y_size), x_size, y_size, dp_size // 2, 2),
        ("zh", "x", "y", "zl", "c"),
    )
    tokens = P(DP_AXES, SEQ_AXES, None)
    in_specs = (tokens, tokens, tokens, tokens, P(DP_AXES, SEQ_AXES), P(), P())
    out_specs = (tokens, tokens, tokens, P(), P())
    return jax.shard_map(shards, mesh=fine, in_specs=in_specs, out_specs=out_specs, check_vma=False)
```

```python
import jax
import jax.numpy as jnp
from jax import lax
from jax.sharding import PartitionSpec as P

HEAD_SIZE = 128
QUERY_HEADS = 16
KEY_VALUE_HEADS = 8
WINDOW_LENGTH = 1024


rope_base = 10000.0
score_scale = 168.0 ** (-0.5)
norm_eps = 1e-06


SEQ_AXES = ("zh", "x", "y")
DP_AXES = ("zl", "c")


def shift(value, steps, cyclic):
    count = lax.axis_size(SEQ_AXES)
    if cyclic:
        pairs = [(source, (source + steps) % count) for source in range(count)]
    else:
        pairs = [(source, source + steps) for source in range(max(0, -steps), min(count, count - steps))]
    return lax.ppermute(value, SEQ_AXES, pairs)


def rotary(field, positions):
    half = field.shape[-1] // 2
    freqs = rope_base ** (-jnp.arange(half, dtype=field.dtype) * 2.0 / field.shape[-1])
    angles = positions.astype(field.dtype)[:, None] * freqs[None, :]
    cosine = jnp.cos(angles)[:, None, :]
    sine = jnp.sin(angles)[:, None, :]
    first = field[..., :half]
    second = field[..., half:]
    return jnp.concatenate(
        [first * cosine - second * sine, second * cosine + first * sine], axis=-1
    )


def prepare(raw, gain, positions):
    meansq = jnp.mean(raw * raw, axis=-1, keepdims=True)
    normed = raw * lax.rsqrt(meansq + norm_eps) * gain
    return rotary(normed, positions)


def attend(query_blk, key_blk, value_blk, gradient_block, allowed):
    scores = (
        jnp.einsum("tgrd,wgd->grtw", query_blk, key_blk, preferred_element_type=jnp.float32)
        * score_scale
    )
    expd = jnp.where(allowed, jnp.exp(scores), 0.0)
    weights = expd / jnp.sum(expd, axis=-1, keepdims=True)
    weights_b = weights.astype(jnp.bfloat16)
    attention_probs = jnp.einsum(
        "grtw,wgd->tgrd", weights_b, value_blk, preferred_element_type=jnp.float32
    )
    delta_rows = jnp.einsum("jwkp,jwkp->wkj", gradient_block.astype(jnp.float32), attention_probs)
    dweights = jnp.einsum(
        "tgrd,wgd->grtw", gradient_block, value_blk, preferred_element_type=jnp.float32
    )
    dscores = (weights * (dweights - delta_rows[..., None])).astype(jnp.bfloat16)
    dquery = score_scale * jnp.einsum(
        "grtw,wgd->tgrd", dscores, key_blk, preferred_element_type=jnp.float32
    )
    dkey = score_scale * jnp.einsum(
        "grtw,tgrd->gwd", dscores, query_blk, preferred_element_type=jnp.float32
    )
    dvalue = jnp.einsum(
        "grtw,tgrd->gwd", weights_b, gradient_block, preferred_element_type=jnp.float32
    )
    return (dquery, dkey, dvalue)


def shards(query_proj, key_projection, value_proj, attn_grad, doc_ids, query_gain, key_norm_gain):
    row_count = query_proj.shape[1]
    behind = WINDOW_LENGTH // row_count
    group_ratio = QUERY_HEADS // KEY_VALUE_HEADS
    group_count = KEY_VALUE_HEADS // 2
    key_span_width = KEY_VALUE_HEADS * HEAD_SIZE
    base = lax.axis_index(SEQ_AXES) * row_count
    local = jnp.arange(row_count, dtype=jnp.int32)
    positions = base + local
    doc_row = doc_ids[0]

    def prepare_function(raw, gain):
        return prepare(raw, gain, positions)

    query_normalized, query_back = jax.vjp(
        prepare_function,
        query_proj[0].astype(jnp.float32).reshape(row_count, QUERY_HEADS, HEAD_SIZE),
        query_gain,
    )
    query_rot = query_normalized.astype(jnp.bfloat16)
    value_flat = value_proj[0]
    doc_rows = jnp.zeros((16, 2 * key_span_width), jnp.bfloat16)
    doc_rows = doc_rows.at[0, :row_count].set(doc_row.astype(jnp.bfloat16))
    packed = jnp.concatenate(
        [jnp.concatenate([key_projection[0], value_flat], axis=1), doc_rows], axis=0
    )
    half = behind // 2
    near, far = [], []
    a_slot, b_slot = packed, packed
    for step in range(half):
        a_slot = shift(a_slot, 1, False)
        b_slot = shift(b_slot, behind if step == 0 else -1, True)
        near.append(a_slot)
        far.append(b_slot)
    window = far + near[::-1] + [packed]
    width = (behind + 1) * row_count
    key_pos = base - behind * row_count + jnp.arange(width, dtype=jnp.int32)
    key_parts, key_backs = [], []
    for index, slab in enumerate(window):
        slab_pos = key_pos[index * row_count:(index + 1) * row_count]

        def prepare_slab(raw, gain, slab_pos=slab_pos):
            return prepare(raw, gain, slab_pos)

        raw = slab[:row_count, :key_span_width].astype(jnp.float32)
        normalized, back = jax.vjp(
            prepare_slab, raw.reshape(row_count, KEY_VALUE_HEADS, HEAD_SIZE), key_norm_gain
        )
        key_parts.append(normalized.astype(jnp.bfloat16))
        key_backs.append(back)
    key_win = jnp.concatenate(key_parts, axis=0)
    value_win = jnp.concatenate(
        [slab[:row_count, key_span_width:] for slab in window], axis=0
    ).reshape(width, KEY_VALUE_HEADS, HEAD_SIZE)
    key_doc = jnp.concatenate([slab[row_count, :row_count] for slab in window]).astype(jnp.int32)
    allowed = (
        (key_pos[None, :] <= positions[:, None])
        & (positions[:, None] - key_pos[None, :] < WINDOW_LENGTH)
        & (key_pos[None, :] >= 0)
        & (key_doc[None, :] == doc_row[:, None])
    )
    dquery_rot, dkey_win, dvalue_win = attend(
        query_rot.reshape(row_count, KEY_VALUE_HEADS, group_ratio, HEAD_SIZE),
        key_win,
        value_win,
        attn_grad[0].reshape(row_count, KEY_VALUE_HEADS, group_ratio, HEAD_SIZE),
        allowed,
    )
    dquery_rot = dquery_rot.reshape(row_count, QUERY_HEADS, HEAD_SIZE)
    dkey_slots = dkey_win.reshape(KEY_VALUE_HEADS, behind + 1, row_count, HEAD_SIZE)
    dvalue_slots = dvalue_win.reshape(KEY_VALUE_HEADS, behind + 1, row_count, HEAD_SIZE)

    def part(slot):
        return jnp.stack([dkey_slots[:, slot], dvalue_slots[:, slot]])

    key_gain_gradient = None
    for slot in range(behind + 1):
        owned = dkey_slots[:, slot]
        if slot < behind:
            owned = owned.astype(jnp.bfloat16).astype(jnp.float32)
        _, gain_part = key_backs[slot](owned.transpose(1, 0, 2))
        key_gain_gradient = gain_part if key_gain_gradient is None else key_gain_gradient + gain_part
    query_raw_gradient, query_gain_gradient = query_back(dquery_rot)
    carry_near = part(behind - half).astype(jnp.bfloat16)
    for offset in range(half - 1, 0, -1):
        got = shift(carry_near, -1, False).astype(jnp.float32)
        carry_near = (got + part(behind - offset)).astype(jnp.bfloat16)
    carry_far = part(behind - half - 1).astype(jnp.bfloat16)
    for offset in range(half + 2, behind + 1):
        got = shift(carry_far, 1, True).astype(jnp.float32)
        carry_far = (got + part(behind - offset)).astype(jnp.bfloat16)
    sent = [shift(carry_near, -1, False), shift(carry_far, -behind, True)]
    gains = (query_gain_gradient, key_gain_gradient)
    for axis in ("y", "x", "zh", "zl", "c"):
        gains = lax.psum(gains, axis)
    gain_query, gain_key = gains
    total = part(behind)
    for moved in sent:
        total = total + moved.astype(jnp.float32)
    key_full_length = total[0].transpose(1, 0, 2).reshape(row_count, key_span_width)
    value_total = total[1].transpose(1, 0, 2).reshape(row_count, key_span_width)
    key_backward = key_backs[behind]
    key_raw_gradient, _ = key_backward(
        key_full_length.reshape(row_count, KEY_VALUE_HEADS, HEAD_SIZE)
    )
    return (
        query_raw_gradient.astype(jnp.bfloat16).reshape(1, row_count, QUERY_HEADS * HEAD_SIZE),
        key_raw_gradient.astype(jnp.bfloat16).reshape(1, row_count, key_span_width),
        value_total.astype(jnp.bfloat16)[None],
        gain_query,
        gain_key,
    )


def solution(mesh):
    seq_size, dp_size = mesh.shape["seq"], mesh.shape["dp"]
    y_size = 8
    x_size = 4
    fine = jax.sharding.Mesh(
        mesh.devices.reshape(seq_size // (x_size * y_size), x_size, y_size, dp_size // 2, 2),
        ("zh", "x", "y", "zl", "c"),
    )
    tokens = P(DP_AXES, SEQ_AXES, None)
    in_specs = (tokens, tokens, tokens, tokens, P(DP_AXES, SEQ_AXES), P(), P())
    out_specs = (tokens, tokens, tokens, P(), P())
    return jax.shard_map(shards, mesh=fine, in_specs=in_specs, out_specs=out_specs, check_vma=False)
```

```python
import jax
import jax.numpy as jnp
from jax import lax
from jax.sharding import PartitionSpec as P

HEAD_SIZE = 128
QUERY_HEADS = 16
KEY_VALUE_HEADS = 8
WINDOW_LENGTH = 1024


rope_base = 10000.0
score_scale = 168.0 ** (-0.5)
norm_eps = 1e-06


SEQ_AXES = ("zh", "x", "y")
DP_AXES = ("zl", "c")


def shift(value, steps, cyclic):
    count = lax.axis_size(SEQ_AXES)
    if cyclic:
        pairs = [(source, (source + steps) % count) for source in range(count)]
    else:
        pairs = [(source, source + steps) for source in range(max(0, -steps), min(count, count - steps))]
    return lax.ppermute(value, SEQ_AXES, pairs)


def rotary(field, positions):
    half = field.shape[-1] // 2
    freqs = rope_base ** (-jnp.arange(half, dtype=field.dtype) * 2.0 / field.shape[-1])
    angles = positions.astype(field.dtype)[:, None] * freqs[None, :]
    cosine = jnp.cos(angles)[:, None, :]
    sine = jnp.sin(angles)[:, None, :]
    first = field[..., :half]
    second = field[..., half:]
    return jnp.concatenate(
        [first * cosine - second * sine, second * cosine + first * sine], axis=-1
    )


def prepare(raw, gain, positions):
    meansq = jnp.mean(raw * raw, axis=-1, keepdims=True)
    normed = raw * lax.rsqrt(meansq + norm_eps) * gain
    return rotary(normed, positions)


def attend(query_blk, key_blk, value_blk, gradient_block, allowed):
    scores = (
        jnp.einsum("tgrd,wgd->grtw", query_blk, key_blk, preferred_element_type=jnp.float32)
        * score_scale
    )
    expd = jnp.where(allowed, jnp.exp(scores), 0.0)
    weights = expd / jnp.sum(expd, axis=-1, keepdims=True)
    weights_b = weights.astype(jnp.bfloat16)
    attention_probs = jnp.einsum(
        "grtw,wgd->tgrd", weights_b, value_blk, preferred_element_type=jnp.float32
    )
    delta_rows = jnp.einsum("jwkp,jwkp->wkj", gradient_block.astype(jnp.float32), attention_probs)
    dweights = jnp.einsum(
        "tgrd,wgd->grtw", gradient_block, value_blk, preferred_element_type=jnp.float32
    )
    dscores = (weights * (dweights - delta_rows[..., None])).astype(jnp.bfloat16)
    dquery = score_scale * jnp.einsum(
        "grtw,wgd->tgrd", dscores, key_blk, preferred_element_type=jnp.float32
    )
    dkey = score_scale * jnp.einsum(
        "grtw,tgrd->gwd", dscores, query_blk, preferred_element_type=jnp.float32
    )
    dvalue = jnp.einsum(
        "grtw,tgrd->gwd", weights_b, gradient_block, preferred_element_type=jnp.float32
    )
    return (dquery, dkey, dvalue)


def shards(query_proj, key_projection, value_proj, attn_grad, doc_ids, query_gain, key_norm_gain):
    row_count = query_proj.shape[1]
    behind = WINDOW_LENGTH // row_count
    group_ratio = QUERY_HEADS // KEY_VALUE_HEADS
    group_count = KEY_VALUE_HEADS // 2
    key_span_width = KEY_VALUE_HEADS * HEAD_SIZE
    base = lax.axis_index(SEQ_AXES) * row_count
    local = jnp.arange(row_count, dtype=jnp.int32)
    positions = base + local
    doc_row = doc_ids[0]

    def prepare_function(raw, gain):
        return prepare(raw, gain, positions)

    query_normalized, query_back = jax.vjp(
        prepare_function,
        query_proj[0].astype(jnp.float32).reshape(row_count, QUERY_HEADS, HEAD_SIZE),
        query_gain,
    )
    query_rot = query_normalized.astype(jnp.bfloat16)
    value_flat = value_proj[0]
    doc_columns = jnp.zeros((row_count, 128), jnp.bfloat16)
    doc_columns = doc_columns.at[:, 0].set(doc_row.astype(jnp.bfloat16))
    packed = jnp.concatenate([key_projection[0], value_flat, doc_columns], axis=1)
    half = behind // 2
    near, far = [], []
    a_slot, b_slot = packed, packed
    for step in range(half):
        a_slot = shift(a_slot, 1, False)
        b_slot = shift(b_slot, behind if step == 0 else -1, True)
        near.append(a_slot)
        far.append(b_slot)
    stacked = jnp.stack(far + near[::-1] + [packed])
    width = (behind + 1) * row_count
    key_raw_win = stacked[:, :, :key_span_width].reshape(width, KEY_VALUE_HEADS, HEAD_SIZE)
    value_win = stacked[:, :, key_span_width:2 * key_span_width].reshape(
        width, KEY_VALUE_HEADS, HEAD_SIZE
    )
    key_doc = stacked[:, :, 2 * key_span_width].reshape(width).astype(jnp.int32)
    key_pos = base - behind * row_count + jnp.arange(width, dtype=jnp.int32)

    def prepare_window(raw, gain):
        return prepare(raw, gain, key_pos)

    key_normalized_win, key_window_back = jax.vjp(
        prepare_window, key_raw_win.astype(jnp.float32), key_norm_gain
    )
    key_win = key_normalized_win.astype(jnp.bfloat16)
    allowed = (
        (key_pos[None, :] <= positions[:, None])
        & (positions[:, None] - key_pos[None, :] < WINDOW_LENGTH)
        & (key_pos[None, :] >= 0)
        & (key_doc[None, :] == doc_row[:, None])
    )
    dquery_rot, dkey_win, dvalue_win = attend(
        query_rot.reshape(row_count, KEY_VALUE_HEADS, group_ratio, HEAD_SIZE),
        key_win,
        value_win,
        attn_grad[0].reshape(row_count, KEY_VALUE_HEADS, group_ratio, HEAD_SIZE),
        allowed,
    )
    dquery_rot = dquery_rot.reshape(row_count, QUERY_HEADS, HEAD_SIZE)
    slots = jnp.stack([dkey_win, dvalue_win]).reshape(
        2, KEY_VALUE_HEADS, behind + 1, row_count, HEAD_SIZE
    )
    remote = slots[:, :, :behind].astype(jnp.bfloat16)
    owned = jnp.concatenate(
        [remote[0].astype(jnp.float32), slots[0, :, behind:]], axis=1
    ).reshape(KEY_VALUE_HEADS, width, HEAD_SIZE)
    _, key_gain_gradient = key_window_back(owned.transpose(1, 0, 2))
    query_raw_gradient, query_gain_gradient = query_back(dquery_rot)
    carry_near = remote[:, :, behind - half]
    for offset in range(half - 1, 0, -1):
        got = shift(carry_near, -1, False).astype(jnp.float32)
        carry_near = (got + slots[:, :, behind - offset]).astype(jnp.bfloat16)
    carry_far = remote[:, :, behind - half - 1]
    for offset in range(half + 2, behind + 1):
        got = shift(carry_far, 1, True).astype(jnp.float32)
        carry_far = (got + slots[:, :, behind - offset]).astype(jnp.bfloat16)
    sent = [shift(carry_near, -1, False), shift(carry_far, -behind, True)]
    gains = (query_gain_gradient, key_gain_gradient)
    for axis in ("y", "x", "zh", "zl", "c"):
        gains = lax.psum(gains, axis)
    gain_query, gain_key = gains
    total = slots[:, :, behind]
    for moved in sent:
        total = total + moved.astype(jnp.float32)
    key_full_length = total[0].transpose(1, 0, 2).reshape(row_count, key_span_width)
    value_total = total[1].transpose(1, 0, 2).reshape(row_count, key_span_width)
    _, key_backward = jax.vjp(
        prepare_function,
        key_projection[0].astype(jnp.float32).reshape(row_count, KEY_VALUE_HEADS, HEAD_SIZE),
        key_norm_gain,
    )
    key_raw_gradient, _ = key_backward(
        key_full_length.reshape(row_count, KEY_VALUE_HEADS, HEAD_SIZE)
    )
    return (
        query_raw_gradient.astype(jnp.bfloat16).reshape(1, row_count, QUERY_HEADS * HEAD_SIZE),
        key_raw_gradient.astype(jnp.bfloat16).reshape(1, row_count, key_span_width),
        value_total.astype(jnp.bfloat16)[None],
        gain_query,
        gain_key,
    )


def solution(mesh):
    seq_size, dp_size = mesh.shape["seq"], mesh.shape["dp"]
    y_size = 8
    x_size = 4
    fine = jax.sharding.Mesh(
        mesh.devices.reshape(seq_size // (x_size * y_size), x_size, y_size, dp_size // 2, 2),
        ("zh", "x", "y", "zl", "c"),
    )
    tokens = P(DP_AXES, SEQ_AXES, None)
    in_specs = (tokens, tokens, tokens, tokens, P(DP_AXES, SEQ_AXES), P(), P())
    out_specs = (tokens, tokens, tokens, P(), P())
    return jax.shard_map(shards, mesh=fine, in_specs=in_specs, out_specs=out_specs, check_vma=False)
```

```python
import jax
import jax.numpy as jnp
from jax import lax
from jax.sharding import PartitionSpec as P

HEAD_SIZE = 128
QUERY_HEADS = 16
KEY_VALUE_HEADS = 8
WINDOW_LENGTH = 1024


rope_base = 10000.0
score_scale = 168.0 ** (-0.5)
norm_eps = 1e-06


SEQ_AXES = ("zh", "x", "y")
DP_AXES = ("zl", "c")


def shift(value, steps, cyclic):
    count = lax.axis_size(SEQ_AXES)
    if cyclic:
        pairs = [(source, (source + steps) % count) for source in range(count)]
    else:
        pairs = [(source, source + steps) for source in range(max(0, -steps), min(count, count - steps))]
    return lax.ppermute(value, SEQ_AXES, pairs)


def rotary(field, positions):
    half = field.shape[-1] // 2
    freqs = rope_base ** (-jnp.arange(half, dtype=field.dtype) * 2.0 / field.shape[-1])
    angles = positions.astype(field.dtype)[:, None] * freqs[None, :]
    cosine = jnp.cos(angles)[:, None, :]
    sine = jnp.sin(angles)[:, None, :]
    first = field[..., :half]
    second = field[..., half:]
    return jnp.concatenate(
        [first * cosine - second * sine, second * cosine + first * sine], axis=-1
    )


def prepare(raw, gain, positions):
    meansq = jnp.mean(raw * raw, axis=-1, keepdims=True)
    normed = raw * lax.rsqrt(meansq + norm_eps) * gain
    return rotary(normed, positions)


def attend(query_blk, key_blk, value_blk, gradient_block, allowed):
    scores = (
        jnp.einsum("tgrd,wgd->grtw", query_blk, key_blk, preferred_element_type=jnp.float32)
        * score_scale
    )
    expd = jnp.where(allowed, jnp.exp(scores), 0.0)
    weights = expd / jnp.sum(expd, axis=-1, keepdims=True)
    weights_b = weights.astype(jnp.bfloat16)
    attention_probs = jnp.einsum(
        "grtw,wgd->tgrd", weights_b, value_blk, preferred_element_type=jnp.float32
    )
    delta_rows = jnp.einsum("jwkp,jwkp->wkj", gradient_block.astype(jnp.float32), attention_probs)
    dweights = jnp.einsum(
        "tgrd,wgd->grtw", gradient_block, value_blk, preferred_element_type=jnp.float32
    )
    dscores = (weights * (dweights - delta_rows[..., None])).astype(jnp.bfloat16)
    dquery = score_scale * jnp.einsum(
        "grtw,wgd->tgrd", dscores, key_blk, preferred_element_type=jnp.float32
    )
    dkey = score_scale * jnp.einsum(
        "grtw,tgrd->gwd", dscores, query_blk, preferred_element_type=jnp.float32
    )
    dvalue = jnp.einsum(
        "grtw,tgrd->gwd", weights_b, gradient_block, preferred_element_type=jnp.float32
    )
    return (dquery, dkey, dvalue)


def shards(query_proj, key_projection, value_proj, attn_grad, doc_ids, query_gain, key_norm_gain):
    row_count = query_proj.shape[1]
    behind = WINDOW_LENGTH // row_count
    group_ratio = QUERY_HEADS // KEY_VALUE_HEADS
    group_count = KEY_VALUE_HEADS // 2
    key_span_width = KEY_VALUE_HEADS * HEAD_SIZE
    base = lax.axis_index(SEQ_AXES) * row_count
    local = jnp.arange(row_count, dtype=jnp.int32)
    positions = base + local
    doc_row = doc_ids[0]

    def prepare_function(raw, gain):
        return prepare(raw, gain, positions)

    query_normalized, query_back = jax.vjp(
        prepare_function,
        query_proj[0].astype(jnp.float32).reshape(row_count, QUERY_HEADS, HEAD_SIZE),
        query_gain,
    )
    query_rot = query_normalized.astype(jnp.bfloat16)
    value_flat = value_proj[0]
    doc_rows = jnp.zeros((16, 2 * key_span_width), jnp.bfloat16)
    doc_rows = doc_rows.at[0, :row_count].set(doc_row.astype(jnp.bfloat16))
    packed = jnp.concatenate(
        [jnp.concatenate([key_projection[0], value_flat], axis=1), doc_rows], axis=0
    )
    half = behind // 2
    near, far = [], []
    a_slot, b_slot = packed, packed
    for step in range(half):
        a_slot = shift(a_slot, 1, False)
        b_slot = shift(b_slot, behind if step == 0 else -1, True)
        near.append(a_slot)
        far.append(b_slot)
    stacked = jnp.stack(far + near[::-1] + [packed])
    width = (behind + 1) * row_count
    key_raw_win = stacked[:, :row_count, :key_span_width].reshape(width, KEY_VALUE_HEADS, HEAD_SIZE)
    value_win = stacked[:, :row_count, key_span_width:].reshape(width, KEY_VALUE_HEADS, HEAD_SIZE)
    key_doc = stacked[:, row_count, :row_count].reshape(width).astype(jnp.int32)
    key_pos = base - behind * row_count + jnp.arange(width, dtype=jnp.int32)

    def prepare_window(raw, gain):
        return prepare(raw, gain, key_pos)

    key_normalized_win, key_window_back = jax.vjp(
        prepare_window, key_raw_win.astype(jnp.float32), key_norm_gain
    )
    key_win = key_normalized_win.astype(jnp.bfloat16)
    allowed = (
        (key_pos[None, :] <= positions[:, None])
        & (positions[:, None] - key_pos[None, :] < WINDOW_LENGTH)
        & (key_pos[None, :] >= 0)
        & (key_doc[None, :] == doc_row[:, None])
    )
    dquery_rot, dkey_win, dvalue_win = attend(
        query_rot.reshape(row_count, KEY_VALUE_HEADS, group_ratio, HEAD_SIZE),
        key_win,
        value_win,
        attn_grad[0].reshape(row_count, KEY_VALUE_HEADS, group_ratio, HEAD_SIZE),
        allowed,
    )
    dquery_rot = dquery_rot.reshape(row_count, QUERY_HEADS, HEAD_SIZE)
    slots = jnp.stack([dkey_win, dvalue_win]).reshape(
        2, KEY_VALUE_HEADS, behind + 1, row_count, HEAD_SIZE
    )
    remote = slots[:, :, :behind].astype(jnp.bfloat16)
    owned = jnp.concatenate(
        [remote[0].astype(jnp.float32), slots[0, :, behind:]], axis=1
    ).reshape(KEY_VALUE_HEADS, width, HEAD_SIZE)
    _, key_gain_gradient = key_window_back(owned.transpose(1, 0, 2))
    query_raw_gradient, query_gain_gradient = query_back(dquery_rot)
    carry_near = remote[:, :, behind - half]
    for offset in range(half - 1, 0, -1):
        got = shift(carry_near, -1, False).astype(jnp.float32)
        carry_near = (got + slots[:, :, behind - offset]).astype(jnp.bfloat16)
    carry_far = remote[:, :, behind - half - 1]
    for offset in range(half + 2, behind + 1):
        got = shift(carry_far, 1, True).astype(jnp.float32)
        carry_far = (got + slots[:, :, behind - offset]).astype(jnp.bfloat16)
    sent = [shift(carry_near, -1, False), shift(carry_far, -behind, True)]
    gains = (query_gain_gradient, key_gain_gradient)
    for axis in ("c", "zl", "y", "x", "zh"):
        gains = lax.psum(gains, axis)
    gain_query, gain_key = gains
    total = slots[:, :, behind]
    for moved in sent:
        total = total + moved.astype(jnp.float32)
    key_full_length = total[0].transpose(1, 0, 2).reshape(row_count, key_span_width)
    value_total = total[1].transpose(1, 0, 2).reshape(row_count, key_span_width)
    _, key_backward = jax.vjp(
        prepare_function,
        key_projection[0].astype(jnp.float32).reshape(row_count, KEY_VALUE_HEADS, HEAD_SIZE),
        key_norm_gain,
    )
    key_raw_gradient, _ = key_backward(
        key_full_length.reshape(row_count, KEY_VALUE_HEADS, HEAD_SIZE)
    )
    return (
        query_raw_gradient.astype(jnp.bfloat16).reshape(1, row_count, QUERY_HEADS * HEAD_SIZE),
        key_raw_gradient.astype(jnp.bfloat16).reshape(1, row_count, key_span_width),
        value_total.astype(jnp.bfloat16)[None],
        gain_query,
        gain_key,
    )


def solution(mesh):
    seq_size, dp_size = mesh.shape["seq"], mesh.shape["dp"]
    y_size = 8
    x_size = 4
    fine = jax.sharding.Mesh(
        mesh.devices.reshape(seq_size // (x_size * y_size), x_size, y_size, dp_size // 2, 2),
        ("zh", "x", "y", "zl", "c"),
    )
    tokens = P(DP_AXES, SEQ_AXES, None)
    in_specs = (tokens, tokens, tokens, tokens, P(DP_AXES, SEQ_AXES), P(), P())
    out_specs = (tokens, tokens, tokens, P(), P())
    return jax.shard_map(shards, mesh=fine, in_specs=in_specs, out_specs=out_specs, check_vma=False)
```

```python
import jax
import jax.numpy as jnp
from jax import lax
from jax.sharding import PartitionSpec as P

HEAD_SIZE = 128
QUERY_HEADS = 16
KEY_VALUE_HEADS = 8
WINDOW_LENGTH = 1024


rope_base = 10000.0
score_scale = 168.0 ** (-0.5)
norm_eps = 1e-06


SEQ_AXES = ("zh", "x", "y")
DP_AXES = ("zl", "c")


def shift(value, steps, cyclic):
    count = lax.axis_size(SEQ_AXES)
    if cyclic:
        pairs = [(source, (source + steps) % count) for source in range(count)]
    else:
        pairs = [(source, source + steps) for source in range(max(0, -steps), min(count, count - steps))]
    return lax.ppermute(value, SEQ_AXES, pairs)


def rotary(field, positions):
    half = field.shape[-1] // 2
    freqs = rope_base ** (-jnp.arange(half, dtype=field.dtype) * 2.0 / field.shape[-1])
    angles = positions.astype(field.dtype)[:, None] * freqs[None, :]
    cosine = jnp.cos(angles)[:, None, :]
    sine = jnp.sin(angles)[:, None, :]
    first = field[..., :half]
    second = field[..., half:]
    return jnp.concatenate(
        [first * cosine - second * sine, second * cosine + first * sine], axis=-1
    )


def prepare(raw, gain, positions):
    meansq = jnp.mean(raw * raw, axis=-1, keepdims=True)
    normed = raw * lax.rsqrt(meansq + norm_eps) * gain
    return rotary(normed, positions)


def attend(query_blk, key_blk, value_blk, gradient_block, allowed):
    scores = (
        jnp.einsum("tgrd,wgd->grtw", query_blk, key_blk, preferred_element_type=jnp.float32)
        * score_scale
    )
    expd = jnp.where(allowed, jnp.exp(scores), 0.0)
    weights = expd / jnp.sum(expd, axis=-1, keepdims=True)
    weights_b = weights.astype(jnp.bfloat16)
    attention_probs = jnp.einsum(
        "grtw,wgd->tgrd", weights_b, value_blk, preferred_element_type=jnp.float32
    )
    delta_rows = jnp.einsum("jwkp,jwkp->wkj", gradient_block.astype(jnp.float32), attention_probs)
    dweights = jnp.einsum(
        "tgrd,wgd->grtw", gradient_block, value_blk, preferred_element_type=jnp.float32
    )
    dscores = (weights * (dweights - delta_rows[..., None])).astype(jnp.bfloat16)
    dquery = score_scale * jnp.einsum(
        "grtw,wgd->tgrd", dscores, key_blk, preferred_element_type=jnp.float32
    )
    dkey = score_scale * jnp.einsum(
        "grtw,tgrd->gwd", dscores, query_blk, preferred_element_type=jnp.float32
    )
    dvalue = jnp.einsum(
        "grtw,tgrd->gwd", weights_b, gradient_block, preferred_element_type=jnp.float32
    )
    return (dquery, dkey, dvalue)


def shards(query_proj, key_projection, value_proj, attn_grad, doc_ids, query_gain, key_norm_gain):
    row_count = query_proj.shape[1]
    behind = WINDOW_LENGTH // row_count
    group_ratio = QUERY_HEADS // KEY_VALUE_HEADS
    group_count = KEY_VALUE_HEADS // 2
    key_span_width = KEY_VALUE_HEADS * HEAD_SIZE
    base = lax.axis_index(SEQ_AXES) * row_count
    local = jnp.arange(row_count, dtype=jnp.int32)
    positions = base + local
    doc_row = doc_ids[0]

    def prepare_function(raw, gain):
        return prepare(raw, gain, positions)

    query_normalized, query_back = jax.vjp(
        prepare_function,
        query_proj[0].astype(jnp.float32).reshape(row_count, QUERY_HEADS, HEAD_SIZE),
        query_gain,
    )
    query_rot = query_normalized.astype(jnp.bfloat16)
    value_flat = value_proj[0]
    doc_rows = jnp.zeros((16, 2 * key_span_width), jnp.bfloat16)
    doc_rows = doc_rows.at[0, :row_count].set(doc_row.astype(jnp.bfloat16))
    packed = jnp.concatenate(
        [jnp.concatenate([key_projection[0], value_flat], axis=1), doc_rows], axis=0
    )
    half = behind // 2
    near, far = [], []
    a_slot, b_slot = packed, packed
    for step in range(half):
        a_slot = shift(a_slot, 1, False)
        b_slot = shift(b_slot, behind if step == 0 else -1, True)
        near.append(a_slot)
        far.append(b_slot)
    stacked = jnp.stack(far + near[::-1] + [packed])
    width = (behind + 1) * row_count
    key_raw_win = stacked[:, :row_count, :key_span_width].reshape(width, KEY_VALUE_HEADS, HEAD_SIZE)
    value_win = stacked[:, :row_count, key_span_width:].reshape(width, KEY_VALUE_HEADS, HEAD_SIZE)
    key_doc = stacked[:, row_count, :row_count].reshape(width).astype(jnp.int32)
    key_pos = base - behind * row_count + jnp.arange(width, dtype=jnp.int32)

    def prepare_window(raw, gain):
        return prepare(raw, gain, key_pos)

    key_normalized_win, key_window_back = jax.vjp(
        prepare_window, key_raw_win.astype(jnp.float32), key_norm_gain
    )
    key_win = key_normalized_win.astype(jnp.bfloat16)
    allowed = (
        (key_pos[None, :] <= positions[:, None])
        & (positions[:, None] - key_pos[None, :] < WINDOW_LENGTH)
        & (key_pos[None, :] >= 0)
        & (key_doc[None, :] == doc_row[:, None])
    )
    dquery_rot, dkey_win, dvalue_win = attend(
        query_rot.reshape(row_count, KEY_VALUE_HEADS, group_ratio, HEAD_SIZE),
        key_win,
        value_win,
        attn_grad[0].reshape(row_count, KEY_VALUE_HEADS, group_ratio, HEAD_SIZE),
        allowed,
    )
    dquery_rot = dquery_rot.reshape(row_count, QUERY_HEADS, HEAD_SIZE)
    slots = jnp.stack([dkey_win, dvalue_win]).reshape(
        2, KEY_VALUE_HEADS, behind + 1, row_count, HEAD_SIZE
    )
    remote = slots[:, :, :behind].astype(jnp.bfloat16)
    owned = jnp.concatenate(
        [remote[0].astype(jnp.float32), slots[0, :, behind:]], axis=1
    ).reshape(KEY_VALUE_HEADS, width, HEAD_SIZE)
    _, key_gain_gradient = key_window_back(owned.transpose(1, 0, 2))
    query_raw_gradient, query_gain_gradient = query_back(dquery_rot)
    carry_near = remote[:, :, behind - half]
    for offset in range(half - 1, 0, -1):
        got = shift(carry_near, -1, False).astype(jnp.float32)
        carry_near = (got + slots[:, :, behind - offset]).astype(jnp.bfloat16)
    carry_far = remote[:, :, behind - half - 1]
    for offset in range(half + 2, behind + 1):
        got = shift(carry_far, 1, True).astype(jnp.float32)
        carry_far = (got + slots[:, :, behind - offset]).astype(jnp.bfloat16)
    sent = [shift(carry_near, -1, False), shift(carry_far, -behind, True)]
    gains = (query_gain_gradient, key_gain_gradient)
    for axis in ("y", "x", "zh", DP_AXES):
        gains = lax.psum(gains, axis)
    gain_query, gain_key = gains
    total = slots[:, :, behind]
    for moved in sent:
        total = total + moved.astype(jnp.float32)
    key_full_length = total[0].transpose(1, 0, 2).reshape(row_count, key_span_width)
    value_total = total[1].transpose(1, 0, 2).reshape(row_count, key_span_width)
    _, key_backward = jax.vjp(
        prepare_function,
        key_projection[0].astype(jnp.float32).reshape(row_count, KEY_VALUE_HEADS, HEAD_SIZE),
        key_norm_gain,
    )
    key_raw_gradient, _ = key_backward(
        key_full_length.reshape(row_count, KEY_VALUE_HEADS, HEAD_SIZE)
    )
    return (
        query_raw_gradient.astype(jnp.bfloat16).reshape(1, row_count, QUERY_HEADS * HEAD_SIZE),
        key_raw_gradient.astype(jnp.bfloat16).reshape(1, row_count, key_span_width),
        value_total.astype(jnp.bfloat16)[None],
        gain_query,
        gain_key,
    )


def solution(mesh):
    seq_size, dp_size = mesh.shape["seq"], mesh.shape["dp"]
    y_size = 8
    x_size = 4
    fine = jax.sharding.Mesh(
        mesh.devices.reshape(seq_size // (x_size * y_size), x_size, y_size, dp_size // 2, 2),
        ("zh", "x", "y", "zl", "c"),
    )
    tokens = P(DP_AXES, SEQ_AXES, None)
    in_specs = (tokens, tokens, tokens, tokens, P(DP_AXES, SEQ_AXES), P(), P())
    out_specs = (tokens, tokens, tokens, P(), P())
    return jax.shard_map(shards, mesh=fine, in_specs=in_specs, out_specs=out_specs, check_vma=False)
```

```python
import jax
import jax.numpy as jnp
from jax import lax
from jax.sharding import PartitionSpec as P

HEAD_SIZE = 128
QUERY_HEADS = 16
KEY_VALUE_HEADS = 8
WINDOW_LENGTH = 1024


rope_base = 10000.0
score_scale = 168.0 ** (-0.5)
norm_eps = 1e-06


SEQ_AXES = ("zh", "x", "y")
DP_AXES = ("zl", "c")


def shift(value, steps, cyclic):
    count = lax.axis_size(SEQ_AXES)
    if cyclic:
        pairs = [(source, (source + steps) % count) for source in range(count)]
    else:
        pairs = [(source, source + steps) for source in range(max(0, -steps), min(count, count - steps))]
    return lax.ppermute(value, SEQ_AXES, pairs)


def rotary(field, positions):
    half = field.shape[-1] // 2
    freqs = rope_base ** (-jnp.arange(half, dtype=field.dtype) * 2.0 / field.shape[-1])
    angles = positions.astype(field.dtype)[:, None] * freqs[None, :]
    cosine = jnp.cos(angles)[:, None, :]
    sine = jnp.sin(angles)[:, None, :]
    first = field[..., :half]
    second = field[..., half:]
    return jnp.concatenate(
        [first * cosine - second * sine, second * cosine + first * sine], axis=-1
    )


def prepare(raw, gain, positions):
    meansq = jnp.mean(raw * raw, axis=-1, keepdims=True)
    normed = raw * lax.rsqrt(meansq + norm_eps) * gain
    return rotary(normed, positions)


def attend(query_blk, key_blk, value_blk, gradient_block, allowed):
    scores = (
        jnp.einsum("tgrd,wgd->grtw", query_blk, key_blk, preferred_element_type=jnp.float32)
        * score_scale
    )
    expd = jnp.where(allowed, jnp.exp(scores), 0.0)
    weights = expd / jnp.sum(expd, axis=-1, keepdims=True)
    weights_b = weights.astype(jnp.bfloat16)
    attention_probs = jnp.einsum(
        "grtw,wgd->tgrd", weights_b, value_blk, preferred_element_type=jnp.float32
    )
    delta_rows = jnp.einsum("jwkp,jwkp->wkj", gradient_block.astype(jnp.float32), attention_probs)
    dweights = jnp.einsum(
        "tgrd,wgd->grtw", gradient_block, value_blk, preferred_element_type=jnp.float32
    )
    dscores = (weights * (dweights - delta_rows[..., None])).astype(jnp.bfloat16)
    dquery = score_scale * jnp.einsum(
        "grtw,wgd->tgrd", dscores, key_blk, preferred_element_type=jnp.float32
    )
    dkey = score_scale * jnp.einsum(
        "grtw,tgrd->gwd", dscores, query_blk, preferred_element_type=jnp.float32
    )
    dvalue = jnp.einsum(
        "grtw,tgrd->gwd", weights_b, gradient_block, preferred_element_type=jnp.float32
    )
    return (dquery, dkey, dvalue)


def shards(query_proj, key_projection, value_proj, attn_grad, doc_ids, query_gain, key_norm_gain):
    row_count = query_proj.shape[1]
    behind = WINDOW_LENGTH // row_count
    group_ratio = QUERY_HEADS // KEY_VALUE_HEADS
    group_count = KEY_VALUE_HEADS // 2
    key_span_width = KEY_VALUE_HEADS * HEAD_SIZE
    base = lax.axis_index(SEQ_AXES) * row_count
    local = jnp.arange(row_count, dtype=jnp.int32)
    positions = base + local
    doc_row = doc_ids[0]

    def prepare_function(raw, gain):
        return prepare(raw, gain, positions)

    query_normalized, query_back = jax.vjp(
        prepare_function,
        query_proj[0].astype(jnp.float32).reshape(row_count, QUERY_HEADS, HEAD_SIZE),
        query_gain,
    )
    query_rot = query_normalized.astype(jnp.bfloat16)
    value_flat = value_proj[0]
    doc_rows = jnp.zeros((16, 2 * key_span_width), jnp.bfloat16)
    doc_rows = doc_rows.at[0, :row_count].set(doc_row.astype(jnp.bfloat16))
    packed = jnp.concatenate(
        [jnp.concatenate([key_projection[0], value_flat], axis=1), doc_rows], axis=0
    )
    half = behind // 2
    near, far = [], []
    a_slot, b_slot = packed, packed
    for step in range(half):
        a_slot = shift(a_slot, 1, False)
        b_slot = shift(b_slot, behind if step == 0 else -1, True)
        near.append(a_slot)
        far.append(b_slot)
    stacked = jnp.stack(far + near[::-1] + [packed])
    width = (behind + 1) * row_count
    key_raw_win = stacked[:, :row_count, :key_span_width].reshape(width, KEY_VALUE_HEADS, HEAD_SIZE)
    value_win = stacked[:, :row_count, key_span_width:].reshape(width, KEY_VALUE_HEADS, HEAD_SIZE)
    key_doc = stacked[:, row_count, :row_count].reshape(width).astype(jnp.int32)
    key_pos = base - behind * row_count + jnp.arange(width, dtype=jnp.int32)

    def prepare_window(raw, gain):
        return prepare(raw, gain, key_pos)

    key_normalized_win, key_window_back = jax.vjp(
        prepare_window, key_raw_win.astype(jnp.float32), key_norm_gain
    )
    key_win = key_normalized_win.astype(jnp.bfloat16)
    allowed = (
        (key_pos[None, :] <= positions[:, None])
        & (positions[:, None] - key_pos[None, :] < WINDOW_LENGTH)
        & (key_pos[None, :] >= 0)
        & (key_doc[None, :] == doc_row[:, None])
    )
    dquery_rot, dkey_win, dvalue_win = attend(
        query_rot.reshape(row_count, KEY_VALUE_HEADS, group_ratio, HEAD_SIZE),
        key_win,
        value_win,
        attn_grad[0].reshape(row_count, KEY_VALUE_HEADS, group_ratio, HEAD_SIZE),
        allowed,
    )
    dquery_rot = dquery_rot.reshape(row_count, QUERY_HEADS, HEAD_SIZE)
    slots = jnp.stack([dkey_win, dvalue_win]).reshape(
        2, KEY_VALUE_HEADS, behind + 1, row_count, HEAD_SIZE
    )
    remote = slots[:, :, :behind].astype(jnp.bfloat16)
    owned = jnp.concatenate(
        [remote[0].astype(jnp.float32), slots[0, :, behind:]], axis=1
    ).reshape(KEY_VALUE_HEADS, width, HEAD_SIZE)
    _, key_gain_gradient = key_window_back(owned.transpose(1, 0, 2))
    query_raw_gradient, query_gain_gradient = query_back(dquery_rot)
    carry_near = remote[:, :, behind - half]
    for offset in range(half - 1, 0, -1):
        got = shift(carry_near, -1, False).astype(jnp.float32)
        carry_near = (got + slots[:, :, behind - offset]).astype(jnp.bfloat16)
    carry_far = remote[:, :, behind - half - 1]
    for offset in range(half + 2, behind + 1):
        got = shift(carry_far, 1, True).astype(jnp.float32)
        carry_far = (got + slots[:, :, behind - offset]).astype(jnp.bfloat16)
    sent = [shift(carry_near, -1, False), shift(carry_far, -behind, True)]
    gains = (query_gain_gradient, key_gain_gradient)
    for axis in ("y", "x", ("zh",) + DP_AXES):
        gains = lax.psum(gains, axis)
    gain_query, gain_key = gains
    total = slots[:, :, behind]
    for moved in sent:
        total = total + moved.astype(jnp.float32)
    key_full_length = total[0].transpose(1, 0, 2).reshape(row_count, key_span_width)
    value_total = total[1].transpose(1, 0, 2).reshape(row_count, key_span_width)
    _, key_backward = jax.vjp(
        prepare_function,
        key_projection[0].astype(jnp.float32).reshape(row_count, KEY_VALUE_HEADS, HEAD_SIZE),
        key_norm_gain,
    )
    key_raw_gradient, _ = key_backward(
        key_full_length.reshape(row_count, KEY_VALUE_HEADS, HEAD_SIZE)
    )
    return (
        query_raw_gradient.astype(jnp.bfloat16).reshape(1, row_count, QUERY_HEADS * HEAD_SIZE),
        key_raw_gradient.astype(jnp.bfloat16).reshape(1, row_count, key_span_width),
        value_total.astype(jnp.bfloat16)[None],
        gain_query,
        gain_key,
    )


def solution(mesh):
    seq_size, dp_size = mesh.shape["seq"], mesh.shape["dp"]
    y_size = 8
    x_size = 4
    fine = jax.sharding.Mesh(
        mesh.devices.reshape(seq_size // (x_size * y_size), x_size, y_size, dp_size // 2, 2),
        ("zh", "x", "y", "zl", "c"),
    )
    tokens = P(DP_AXES, SEQ_AXES, None)
    in_specs = (tokens, tokens, tokens, tokens, P(DP_AXES, SEQ_AXES), P(), P())
    out_specs = (tokens, tokens, tokens, P(), P())
    return jax.shard_map(shards, mesh=fine, in_specs=in_specs, out_specs=out_specs, check_vma=False)
```
